32 devices in a mesh: row: 8 (over y, x, core), col: 4 (over z).
Axes of the slice: x: 2, y: 2, z: 4, core: 2. Of those that a mesh axis runs over, the one named last changes fastest.
Arguments:
- image: bfloat16 [512, 512, 128], P('row', 'col'), may hold values from -6 to 6
- raw_first: float32 [15, 15, 128], replicated, may hold values from -0.75 to 0.75
- sigma_first: float32 [128], replicated, may hold values from 2 to 10
- in_first: bfloat16 [128, 512], replicated, may hold values from -0.5 to 0.5
- out_first: bfloat16 [512, 128], replicated, may hold values from -0.25 to 0.25
- widen: bfloat16 [128, 256], replicated, may hold values from -0.75 to 0.75
- raw_second: float32 [15, 15, 256], replicated, may hold values from -0.75 to 0.75
- sigma_second: float32 [256], replicated, may hold values from 2 to 10
- in_second: bfloat16 [256, 1024], replicated, may hold values from -0.375 to 0.375
- out_second: bfloat16 [1024, 256], replicated, may hold values from -0.1875 to 0.1875
Outputs:
- encoded: bfloat16 [128, 128, 256], P('row', 'col')
The draws below stay inside these ranges and needn't reach their ends.
All inputs are finite; a program needn't handle non-finite values.
Results may differ from the reference program's by a relative error of at most 0.0065.
Values may be sent and summed in bfloat16 or wider, within the bound.
No kernel may reach another device: no remote copies, remote signals or barrier semaphores. Data moves between devices by JAX's collectives and lax.ppermute only.
A program may use at most 64 MiB of HBM per device.

```python
import math
import jax
import jax.numpy as jnp
from jax import lax

C1 = 128
HID1 = 512
C2 = 256
HID2 = 1024
KS = 15
TH = 64
H = 512
W = 512


def shard_levels(rng, extent, shards, least, top_value):
    factor_of, own = 1.0, jax.random.fold_in(rng, 6)
    for axis_at, parts in shards:
        steps = jnp.exp(jax.random.uniform(jax.random.fold_in(own, axis_at), (parts,), jnp.float32, least / len(shards), top_value / len(shards)))
        factor_of = factor_of * jnp.repeat(steps, extent[axis_at] // parts).reshape([-1 if axis == axis_at else 1 for axis in range(len(extent))])
    return factor_of


def gaussian(key, extent, deviation, limit, pieces=(), held_as=jnp.bfloat16):
    drawn = jax.random.normal(key, extent, jnp.float32) * deviation
    if len(pieces) > 0:
        drawn = shard_levels(key, extent, pieces, -0.22, 0.18) * drawn
    return jnp.clip(drawn, min=-limit, max=limit).astype(held_as)


def setup_inputs(seed: int = 0) -> dict:
    arg_keys = jax.random.split(jax.random.key(seed), 11)
    return {
        "image": gaussian(arg_keys[0], (H, W, C1), 1.0, 6.0, ((0, 8), (1, 4))),
        "raw_first": gaussian(arg_keys[1], (KS, KS, C1), (KS * KS // 4) ** -0.5, 0.75, (), jnp.float32),
        "sigma_first": jnp.clip(jnp.exp(jax.random.uniform(arg_keys[2], (C1,), jnp.float32, math.log(2.0), math.log(10.0))), 2.0, 10.0),
        "in_first": gaussian(arg_keys[3], (C1, HID1), C1 ** -0.5, 0.5),
        "out_first": gaussian(arg_keys[4], (HID1, C1), HID1 ** -0.5, 0.25),
        "widen": gaussian(arg_keys[5], (C1, C2), (C1 // 2) ** -0.5, 0.75),
        "raw_second": gaussian(arg_keys[6], (KS, KS, C2), (KS * KS // 4) ** -0.5, 0.75, (), jnp.float32),
        "sigma_second": jnp.clip(jnp.exp(jax.random.uniform(arg_keys[7], (C2,), jnp.float32, math.log(2.0), math.log(10.0))), 2.0, 10.0),
        "in_second": gaussian(arg_keys[8], (C2, HID2), C2 ** -0.5, 0.375),
        "out_second": gaussian(arg_keys[9], (HID2, C2), HID2 ** -0.5, 0.1875),
    }


def masked_kernel(raw, sigma):
    offsets = jnp.arange(KS).astype(jnp.float32) - 7.0
    dist = offsets[:, None] ** 2 + offsets[None, :] ** 2
    mask = jnp.exp(-dist[:, :, None] / (2.0 * sigma[None, None, :] ** 2))
    return (raw * mask).astype(jnp.bfloat16)

def depthwise(field, kernel):
    channels = field.shape[2]
    return lax.conv_general_dilated(field[None], kernel[:, :, None, :], (1, 1), ((7, 7), (7, 7)), dimension_numbers=('NHWC', 'HWIO', 'NHWC'), feature_group_count=channels, preferred_element_type=jnp.float32)[0]

def channel_mlp(conv_out, field, w_in, w_out):
    mean = lax.optimization_barrier(jnp.mean(conv_out, axis=-1, keepdims=True))
    var = lax.optimization_barrier(jnp.mean((conv_out - mean) ** 2, axis=-1, keepdims=True))
    normed = ((conv_out - mean) * lax.rsqrt(var + 1e-06)).astype(jnp.bfloat16)
    hidden = jax.nn.gelu(jnp.dot(normed, w_in, preferred_element_type=jnp.float32)).astype(jnp.bfloat16)
    mixed = jnp.dot(hidden, w_out, preferred_element_type=jnp.float32)
    return (field.astype(jnp.float32) + mixed).astype(jnp.bfloat16)

def section(field, raw, sigma, w_in, w_out):
    conv_out = depthwise(field, masked_kernel(raw, sigma))
    band = TH // 2
    rows = field.shape[0]
    conv_bands = conv_out.reshape(rows // band, band, field.shape[1], field.shape[2])
    field_bands = field.reshape(rows // band, band, field.shape[1], field.shape[2])
    result = lax.map(lambda pair: channel_mlp(pair[0], pair[1], w_in, w_out), (conv_bands, field_bands))
    return result.reshape(field.shape)

def blur_down(field):
    padded = jnp.pad(field, ((1, 1), (1, 1), (0, 0))).astype(jnp.float32)
    rows = field.shape[0]
    cols = field.shape[1]
    upper = padded[0:rows].reshape(rows // 2, 2, cols + 2, -1)
    lower = padded[2:rows + 2].reshape(rows // 2, 2, cols + 2, -1)
    vert = (upper[:, 0] + 3.0 * upper[:, 1] + 3.0 * lower[:, 0] + lower[:, 1]) / 8.0
    left = vert[:, 0:cols].reshape(rows // 2, cols // 2, 2, -1)
    right = vert[:, 2:cols + 2].reshape(rows // 2, cols // 2, 2, -1)
    return ((left[:, :, 0] + 3.0 * left[:, :, 1] + 3.0 * right[:, :, 0] + right[:, :, 1]) / 8.0).astype(jnp.bfloat16)

def reference(image, raw_first, sigma_first, in_first, out_first, widen, raw_second, sigma_second, in_second, out_second):
    first = section(image, raw_first, sigma_first, in_first, out_first)
    first_pooled = blur_down(first)
    widened = jnp.dot(first_pooled, widen, preferred_element_type=jnp.float32).astype(jnp.bfloat16)
    second = section(widened, raw_second, sigma_second, in_second, out_second)
    return blur_down(second)
```

```python
import functools

import jax
import jax.numpy as jnp
from jax import lax
from jax.experimental import pallas as pl
from jax.experimental.pallas import tpu as pltpu
from jax.sharding import PartitionSpec as P


def padded_2(block, sides, width):
    for axis, dim in sides:
        count = lax.axis_size(axis)
        forward = [(i, i + 1) for i in range(count - 1)]
        backward = [(target, source) for source, target in forward]
        low = lax.ppermute(
            lax.slice_in_dim(block, block.shape[dim] - width, None, axis=dim), axis, forward
        )
        high = lax.ppermute(lax.slice_in_dim(block, 0, width, axis=dim), axis, backward)
        block = jnp.concatenate([low, block, high], axis=dim)
    return block


def masked_kernel(raw, sigma):
    offsets = jnp.arange(raw.shape[0]).astype(jnp.float32) - 7.0
    dist = offsets[:, None] ** 2 + offsets[None, :] ** 2
    mask = jnp.exp(-dist[:, :, None] / (2.0 * sigma[None, None, :] ** 2))
    return (raw * mask).astype(jnp.bfloat16)


def _dw_body(x_ref, k_ref, o_ref, xs_ref, *, taps, rows, cols, chans, rb):
    nlb = chans // 128
    njb = cols // 8
    nrb = rows // rb
    for b in range(taps):
        def shift(r, c):
            xs_ref[r] = x_ref[r, pl.ds(b, cols), :]
            return c

        lax.fori_loop(0, rows + taps - 1, shift, 0)
        for lb in range(nlb):
            lanes = pl.ds(lb * 128, 128)
            ks = [k_ref[a, b, :, lanes] for a in range(taps)]

            def body(i, c):
                r0 = pl.multiple_of((i // njb) * rb, rb)
                j0 = pl.multiple_of((i % njb) * 8, 8)
                xs = xs_ref[pl.ds(r0, rb + taps - 1), pl.ds(j0, 8), lanes]
                if b == 0:
                    acc = jnp.zeros((rb, 8, 128), jnp.float32)
                else:
                    acc = o_ref[pl.ds(r0, rb), pl.ds(j0, 8), lanes]
                for a in range(taps):
                    acc = acc + xs[a : a + rb] * ks[a][None]
                o_ref[pl.ds(r0, rb), pl.ds(j0, 8), lanes] = acc
                return c

            lax.fori_loop(0, nrb * njb, body, 0)


def depthwise(extended, kernel):
    taps = kernel.shape[0]
    rows = extended.shape[0] - taps + 1
    cols = extended.shape[1] - taps + 1
    chans = extended.shape[2]
    kb = jnp.broadcast_to(kernel.astype(jnp.float32)[:, :, None, :], (taps, taps, 8, chans))
    body = functools.partial(_dw_body, taps=taps, rows=rows, cols=cols, chans=chans, rb=8)
    vmem = pl.BlockSpec(memory_space=pltpu.VMEM)
    return pl.pallas_call(
        body,
        out_shape=jax.ShapeDtypeStruct((rows, cols, chans), jnp.float32),
        in_specs=[vmem, vmem],
        out_specs=vmem,
        scratch_shapes=[pltpu.VMEM((extended.shape[0], cols, chans), jnp.float32)],
        cost_estimate=pl.CostEstimate(
            flops=2 * rows * cols * chans * taps * taps,
            transcendentals=0,
            bytes_accessed=extended.size * 4 + rows * cols * chans * 4,
        ),
    )(extended.astype(jnp.float32), kb)


def local_section(extended, raw, sigma, w_in, w_out):
    kernel = masked_kernel(raw, sigma)
    conv_out = depthwise(extended, kernel)
    field = extended[7 : extended.shape[0] - 7, 7 : extended.shape[1] - 7]
    mean = jnp.mean(conv_out, axis=-1, keepdims=True)
    var = jnp.mean((conv_out - mean) ** 2, axis=-1, keepdims=True)
    normed = ((conv_out - mean) * lax.rsqrt(var + 1e-06)).astype(jnp.bfloat16)
    hidden = jax.nn.gelu(jnp.dot(normed, w_in, preferred_element_type=jnp.float32)).astype(
        jnp.bfloat16
    )
    mixed = jnp.dot(hidden, w_out, preferred_element_type=jnp.float32)
    return (field.astype(jnp.float32) + mixed).astype(jnp.bfloat16)


def blur_down(padded):
    rows = padded.shape[0] - 2
    cols = padded.shape[1] - 2
    padded = padded.astype(jnp.float32)
    upper = padded[0:rows].reshape(rows // 2, 2, cols + 2, -1)
    lower = padded[2 : rows + 2].reshape(rows // 2, 2, cols + 2, -1)
    vert = (upper[:, 0] + 3.0 * upper[:, 1] + 3.0 * lower[:, 0] + lower[:, 1]) / 8.0
    left = vert[:, 0:cols].reshape(rows // 2, cols // 2, 2, -1)
    right = vert[:, 2 : cols + 2].reshape(rows // 2, cols // 2, 2, -1)
    return (
        (left[:, :, 0] + 3.0 * left[:, :, 1] + 3.0 * right[:, :, 0] + right[:, :, 1]) / 8.0
    ).astype(jnp.bfloat16)


def on_device(
    image,
    raw_first,
    sigma_first,
    in_first,
    out_first,
    widen,
    raw_second,
    sigma_second,
    in_second,
    out_second,
):
    reach = 7
    extended = padded_2(image, (("row", 0), ("col", 1)), reach)
    first = local_section(extended, raw_first, sigma_first, in_first, out_first)
    first_cycle = padded_2(first, (("row", 0), ("col", 1)), 1)
    first_pooled = blur_down(first_cycle)
    widened = jnp.dot(first_pooled, widen, preferred_element_type=jnp.float32).astype(jnp.bfloat16)
    widened_ext = padded_2(widened, (("row", 0), ("col", 1)), reach)
    second = local_section(widened_ext, raw_second, sigma_second, in_second, out_second)
    second_cycle = padded_2(second, (("row", 0), ("col", 1)), 1)
    return blur_down(second_cycle)


def solution(mesh):
    placed = (P("row", "col", None), P(), P(), P(), P(), P(), P(), P(), P(), P())
    return jax.shard_map(
        on_device, mesh=mesh, in_specs=placed, out_specs=P("row", "col", None), check_vma=False
    )
```

```python
import functools

import jax
import jax.numpy as jnp
from jax import lax
from jax.experimental import pallas as pl
from jax.experimental.pallas import tpu as pltpu
from jax.sharding import PartitionSpec as P


def padded_2(block, sides, width):
    for axis, dim in sides:
        count = lax.axis_size(axis)
        forward = [(i, i + 1) for i in range(count - 1)]
        backward = [(target, source) for source, target in forward]
        low = lax.ppermute(
            lax.slice_in_dim(block, block.shape[dim] - width, None, axis=dim), axis, forward
        )
        high = lax.ppermute(lax.slice_in_dim(block, 0, width, axis=dim), axis, backward)
        block = jnp.concatenate([low, block, high], axis=dim)
    return block


def masked_kernel(raw, sigma):
    offsets = jnp.arange(raw.shape[0]).astype(jnp.float32) - 7.0
    dist = offsets[:, None] ** 2 + offsets[None, :] ** 2
    mask = jnp.exp(-dist[:, :, None] / (2.0 * sigma[None, None, :] ** 2))
    return (raw * mask).astype(jnp.bfloat16)


def _dw_body(x_ref, k_ref, o_ref, xs_ref, *, taps, rows, cols, chans, rb):
    nlb = chans // 128
    njb = cols // 8
    nrb = rows // rb
    for b in range(taps):
        def shift(r, c):
            xs_ref[r] = x_ref[r, pl.ds(b, cols), :]
            return c

        lax.fori_loop(0, rows + taps - 1, shift, 0)
        for lb in range(nlb):
            lanes = pl.ds(lb * 128, 128)
            ks = [k_ref[a, b, :, lanes] for a in range(taps)]

            def body(i, c):
                r0 = pl.multiple_of((i // njb) * rb, rb)
                j0 = pl.multiple_of((i % njb) * 8, 8)
                xs = xs_ref[pl.ds(r0, rb + taps - 1), pl.ds(j0, 8), lanes]
                if b == 0:
                    acc = jnp.zeros((rb, 8, 128), jnp.float32)
                else:
                    acc = o_ref[pl.ds(r0, rb), pl.ds(j0, 8), lanes]
                terms = [xs[a : a + rb] * ks[a][None] for a in range(taps)]
                for g in range(0, taps, 5):
                    group = terms[g : g + 5]
                    while len(group) > 1:
                        group = [
                            group[i] + group[i + 1] if i + 1 < len(group) else group[i]
                            for i in range(0, len(group), 2)
                        ]
                    acc = acc + group[0]
                o_ref[pl.ds(r0, rb), pl.ds(j0, 8), lanes] = acc
                return c

            lax.fori_loop(0, nrb * njb, body, 0, unroll=2)


def depthwise(extended, kernel):
    taps = kernel.shape[0]
    rows = extended.shape[0] - taps + 1
    cols = extended.shape[1] - taps + 1
    chans = extended.shape[2]
    kb = jnp.broadcast_to(kernel.astype(jnp.float32)[:, :, None, :], (taps, taps, 8, chans))
    body = functools.partial(_dw_body, taps=taps, rows=rows, cols=cols, chans=chans, rb=8)
    vmem = pl.BlockSpec(memory_space=pltpu.VMEM)
    return pl.pallas_call(
        body,
        out_shape=jax.ShapeDtypeStruct((rows, cols, chans), jnp.float32),
        in_specs=[vmem, vmem],
        out_specs=vmem,
        scratch_shapes=[pltpu.VMEM((extended.shape[0], cols, chans), jnp.float32)],
        cost_estimate=pl.CostEstimate(
            flops=2 * rows * cols * chans * taps * taps,
            transcendentals=0,
            bytes_accessed=extended.size * 4 + rows * cols * chans * 4,
        ),
    )(extended.astype(jnp.float32), kb)


def local_section(extended, raw, sigma, w_in, w_out):
    kernel = masked_kernel(raw, sigma)
    conv_out = depthwise(extended, kernel)
    field = extended[7 : extended.shape[0] - 7, 7 : extended.shape[1] - 7]
    mean = jnp.mean(conv_out, axis=-1, keepdims=True)
    var = jnp.mean((conv_out - mean) ** 2, axis=-1, keepdims=True)
    normed = ((conv_out - mean) * lax.rsqrt(var + 1e-06)).astype(jnp.bfloat16)
    hidden = jax.nn.gelu(jnp.dot(normed, w_in, preferred_element_type=jnp.float32)).astype(
        jnp.bfloat16
    )
    mixed = jnp.dot(hidden, w_out, preferred_element_type=jnp.float32)
    return (field.astype(jnp.float32) + mixed).astype(jnp.bfloat16)


def blur_down(padded):
    rows = padded.shape[0] - 2
    cols = padded.shape[1] - 2
    padded = padded.astype(jnp.float32)
    upper = padded[0:rows].reshape(rows // 2, 2, cols + 2, -1)
    lower = padded[2 : rows + 2].reshape(rows // 2, 2, cols + 2, -1)
    vert = (upper[:, 0] + 3.0 * upper[:, 1] + 3.0 * lower[:, 0] + lower[:, 1]) / 8.0
    left = vert[:, 0:cols].reshape(rows // 2, cols // 2, 2, -1)
    right = vert[:, 2 : cols + 2].reshape(rows // 2, cols // 2, 2, -1)
    return (
        (left[:, :, 0] + 3.0 * left[:, :, 1] + 3.0 * right[:, :, 0] + right[:, :, 1]) / 8.0
    ).astype(jnp.bfloat16)


def on_device(
    image,
    raw_first,
    sigma_first,
    in_first,
    out_first,
    widen,
    raw_second,
    sigma_second,
    in_second,
    out_second,
):
    reach = 7
    extended = padded_2(image, (("row", 0), ("col", 1)), reach)
    first = local_section(extended, raw_first, sigma_first, in_first, out_first)
    first_cycle = padded_2(first, (("row", 0), ("col", 1)), 1)
    first_pooled = blur_down(first_cycle)
    widened = jnp.dot(first_pooled, widen, preferred_element_type=jnp.float32).astype(jnp.bfloat16)
    widened_ext = padded_2(widened, (("row", 0), ("col", 1)), reach)
    second = local_section(widened_ext, raw_second, sigma_second, in_second, out_second)
    second_cycle = padded_2(second, (("row", 0), ("col", 1)), 1)
    return blur_down(second_cycle)


def solution(mesh):
    placed = (P("row", "col", None), P(), P(), P(), P(), P(), P(), P(), P(), P())
    return jax.shard_map(
        on_device, mesh=mesh, in_specs=placed, out_specs=P("row", "col", None), check_vma=False
    )
```

```python
import functools

import jax
import jax.numpy as jnp
from jax import lax
from jax.experimental import pallas as pl
from jax.experimental.pallas import tpu as pltpu
from jax.sharding import PartitionSpec as P


def padded_2(block, sides, width):
    for axis, dim in sides:
        count = lax.axis_size(axis)
        forward = [(i, i + 1) for i in range(count - 1)]
        backward = [(target, source) for source, target in forward]
        low = lax.ppermute(
            lax.slice_in_dim(block, block.shape[dim] - width, None, axis=dim), axis, forward
        )
        high = lax.ppermute(lax.slice_in_dim(block, 0, width, axis=dim), axis, backward)
        block = jnp.concatenate([low, block, high], axis=dim)
    return block


def masked_kernel(raw, sigma):
    offsets = jnp.arange(raw.shape[0]).astype(jnp.float32) - 7.0
    dist = offsets[:, None] ** 2 + offsets[None, :] ** 2
    mask = jnp.exp(-dist[:, :, None] / (2.0 * sigma[None, None, :] ** 2))
    return (raw * mask).astype(jnp.bfloat16)


def _dw_body(x_ref, k_ref, o_ref, xs_ref, *, taps, rows, cols, chans, rb):
    nlb = chans // 128
    njb = cols // 8
    nrb = rows // rb
    for b in range(taps):
        def shift(r, c):
            xs_ref[r] = x_ref[r, pl.ds(b, cols), :]
            return c

        lax.fori_loop(0, rows + taps - 1, shift, 0)
        for lb in range(nlb):
            lanes = pl.ds(lb * 128, 128)
            ks = [k_ref[a, b, :, lanes] for a in range(taps)]

            def body(i, c):
                r0 = pl.multiple_of((i // njb) * rb, rb)
                j0 = pl.multiple_of((i % njb) * 8, 8)
                xs = xs_ref[pl.ds(r0, rb + taps - 1), pl.ds(j0, 8), lanes]
                if b == 0:
                    acc = jnp.zeros((rb, 8, 128), jnp.float32)
                else:
                    acc = o_ref[pl.ds(r0, rb), pl.ds(j0, 8), lanes]
                terms = [xs[a : a + rb] * ks[a][None] for a in range(taps)]
                for g in range(0, taps, 5):
                    group = terms[g : g + 5]
                    while len(group) > 1:
                        group = [
                            group[i] + group[i + 1] if i + 1 < len(group) else group[i]
                            for i in range(0, len(group), 2)
                        ]
                    acc = acc + group[0]
                o_ref[pl.ds(r0, rb), pl.ds(j0, 8), lanes] = acc
                return c

            lax.fori_loop(0, nrb * njb, body, 0, unroll=2)


def depthwise(extended, kernel, rb):
    taps = kernel.shape[0]
    rows = extended.shape[0] - taps + 1
    cols = extended.shape[1] - taps + 1
    chans = extended.shape[2]
    rows_p = -(-rows // rb) * rb
    cols_p = -(-cols // 8) * 8
    padded = jnp.pad(
        extended.astype(jnp.float32), ((0, rows_p - rows), (0, cols_p - cols), (0, 0))
    )
    kb = jnp.broadcast_to(kernel.astype(jnp.float32)[:, :, None, :], (taps, taps, 8, chans))
    body = functools.partial(_dw_body, taps=taps, rows=rows_p, cols=cols_p, chans=chans, rb=rb)
    vmem = pl.BlockSpec(memory_space=pltpu.VMEM)
    out = pl.pallas_call(
        body,
        out_shape=jax.ShapeDtypeStruct((rows_p, cols_p, chans), jnp.float32),
        in_specs=[vmem, vmem],
        out_specs=vmem,
        scratch_shapes=[pltpu.VMEM((padded.shape[0], cols_p, chans), jnp.float32)],
        cost_estimate=pl.CostEstimate(
            flops=2 * rows_p * cols_p * chans * taps * taps,
            transcendentals=0,
            bytes_accessed=padded.size * 4 + rows_p * cols_p * chans * 4,
        ),
    )(padded, kb)
    return out[:rows, :cols]


def local_section(extended, raw, sigma, w_in, w_out, rb):
    kernel = masked_kernel(raw, sigma)
    conv_out = depthwise(extended, kernel, rb)
    field = extended[7 : extended.shape[0] - 7, 7 : extended.shape[1] - 7]
    mean = jnp.mean(conv_out, axis=-1, keepdims=True)
    var = jnp.mean((conv_out - mean) ** 2, axis=-1, keepdims=True)
    normed = ((conv_out - mean) * lax.rsqrt(var + 1e-06)).astype(jnp.bfloat16)
    hidden = jax.nn.gelu(jnp.dot(normed, w_in, preferred_element_type=jnp.float32)).astype(
        jnp.bfloat16
    )
    mixed = jnp.dot(hidden, w_out, preferred_element_type=jnp.float32)
    out = (field.astype(jnp.float32) + mixed).astype(jnp.bfloat16)
    return zero_outer_edge(out)


def zero_outer_edge(block):
    keep = None
    for axis, dim in (("row", 0), ("col", 1)):
        index = lax.axis_index(axis)
        last = lax.axis_size(axis) - 1
        pos = lax.broadcasted_iota(jnp.int32, block.shape[:2], dim)
        ok = ((pos != 0) | (index != 0)) & ((pos != block.shape[dim] - 1) | (index != last))
        keep = ok if keep is None else keep & ok
    return jnp.where(keep[:, :, None], block, jnp.zeros_like(block))


def blur_down(padded):
    rows = padded.shape[0] - 2
    cols = padded.shape[1] - 2
    padded = padded.astype(jnp.float32)
    upper = padded[0:rows].reshape(rows // 2, 2, cols + 2, -1)
    lower = padded[2 : rows + 2].reshape(rows // 2, 2, cols + 2, -1)
    vert = (upper[:, 0] + 3.0 * upper[:, 1] + 3.0 * lower[:, 0] + lower[:, 1]) / 8.0
    left = vert[:, 0:cols].reshape(rows // 2, cols // 2, 2, -1)
    right = vert[:, 2 : cols + 2].reshape(rows // 2, cols // 2, 2, -1)
    return (
        (left[:, :, 0] + 3.0 * left[:, :, 1] + 3.0 * right[:, :, 0] + right[:, :, 1]) / 8.0
    ).astype(jnp.bfloat16)


def on_device(
    image,
    raw_first,
    sigma_first,
    in_first,
    out_first,
    widen,
    raw_second,
    sigma_second,
    in_second,
    out_second,
):
    reach = 8
    extended = padded_2(image, (("row", 0), ("col", 1)), reach)
    first_cycle = local_section(extended, raw_first, sigma_first, in_first, out_first, 6)
    first_pooled = blur_down(first_cycle)
    widened = jnp.dot(first_pooled, widen, preferred_element_type=jnp.float32).astype(jnp.bfloat16)
    widened_ext = padded_2(widened, (("row", 0), ("col", 1)), reach)
    second_cycle = local_section(widened_ext, raw_second, sigma_second, in_second, out_second, 6)
    return blur_down(second_cycle)


def solution(mesh):
    placed = (P("row", "col", None), P(), P(), P(), P(), P(), P(), P(), P(), P())
    return jax.shard_map(
        on_device, mesh=mesh, in_specs=placed, out_specs=P("row", "col", None), check_vma=False
    )
```

```python
import functools

import jax
import jax.numpy as jnp
from jax import lax
from jax.experimental import pallas as pl
from jax.experimental.pallas import tpu as pltpu
from jax.sharding import PartitionSpec as P


def _piece(block, d, dim, width):
    if d < 0:
        return lax.slice_in_dim(block, block.shape[dim] - width, None, axis=dim)
    if d > 0:
        return lax.slice_in_dim(block, 0, width, axis=dim)
    return block


def padded_2(block, width):
    nr = lax.axis_size("row")
    nc = lax.axis_size("col")
    got = {}
    for dr in (-1, 0, 1):
        for dc in (-1, 0, 1):
            if dr == 0 and dc == 0:
                continue
            piece = _piece(_piece(block, dr, 0, width), dc, 1, width)
            if dc == 0:
                pairs = [(r, r - dr) for r in range(nr) if 0 <= r - dr < nr]
                got[dr, dc] = lax.ppermute(piece, "row", pairs)
            elif dr == 0:
                pairs = [(c, c - dc) for c in range(nc) if 0 <= c - dc < nc]
                got[dr, dc] = lax.ppermute(piece, "col", pairs)
            else:
                pairs = [
                    (r * nc + c, (r - dr) * nc + (c - dc))
                    for r in range(nr)
                    for c in range(nc)
                    if 0 <= r - dr < nr and 0 <= c - dc < nc
                ]
                got[dr, dc] = lax.ppermute(piece, ("row", "col"), pairs)
    got[0, 0] = block
    bands = [
        jnp.concatenate([got[dr, -1], got[dr, 0], got[dr, 1]], axis=1) for dr in (-1, 0, 1)
    ]
    return jnp.concatenate(bands, axis=0)


def masked_kernel(raw, sigma):
    offsets = jnp.arange(raw.shape[0]).astype(jnp.float32) - 7.0
    dist = offsets[:, None] ** 2 + offsets[None, :] ** 2
    mask = jnp.exp(-dist[:, :, None] / (2.0 * sigma[None, None, :] ** 2))
    return (raw * mask).astype(jnp.bfloat16)


def _dw_body(x_ref, k_ref, o_ref, xs_ref, *, taps, rows, cols, chans, rb):
    nlb = chans // 128
    njb = cols // 8
    nrb = rows // rb
    for b in range(taps):
        def shift(r, c):
            xs_ref[r] = x_ref[r, pl.ds(b, cols), :]
            return c

        lax.fori_loop(0, rows + taps - 1, shift, 0)
        for lb in range(nlb):
            lanes = pl.ds(lb * 128, 128)
            ks = [k_ref[a, b, :, lanes] for a in range(taps)]

            def body(i, c):
                r0 = pl.multiple_of((i // njb) * rb, rb)
                j0 = pl.multiple_of((i % njb) * 8, 8)
                xs = xs_ref[pl.ds(r0, rb + taps - 1), pl.ds(j0, 8), lanes]
                if b == 0:
                    acc = jnp.zeros((rb, 8, 128), jnp.float32)
                else:
                    acc = o_ref[pl.ds(r0, rb), pl.ds(j0, 8), lanes]
                terms = [xs[a : a + rb] * ks[a][None] for a in range(taps)]
                for g in range(0, taps, 5):
                    group = terms[g : g + 5]
                    while len(group) > 1:
                        group = [
                            group[i] + group[i + 1] if i + 1 < len(group) else group[i]
                            for i in range(0, len(group), 2)
                        ]
                    acc = acc + group[0]
                o_ref[pl.ds(r0, rb), pl.ds(j0, 8), lanes] = acc
                return c

            lax.fori_loop(0, nrb * njb, body, 0, unroll=2)


def depthwise(extended, kernel):
    taps = kernel.shape[0]
    rows = extended.shape[0] - taps + 1
    cols = extended.shape[1] - taps + 1
    chans = extended.shape[2]
    kb = jnp.broadcast_to(kernel.astype(jnp.float32)[:, :, None, :], (taps, taps, 8, chans))
    body = functools.partial(_dw_body, taps=taps, rows=rows, cols=cols, chans=chans, rb=8)
    vmem = pl.BlockSpec(memory_space=pltpu.VMEM)
    return pl.pallas_call(
        body,
        out_shape=jax.ShapeDtypeStruct((rows, cols, chans), jnp.float32),
        in_specs=[vmem, vmem],
        out_specs=vmem,
        scratch_shapes=[pltpu.VMEM((extended.shape[0], cols, chans), jnp.float32)],
        cost_estimate=pl.CostEstimate(
            flops=2 * rows * cols * chans * taps * taps,
            transcendentals=0,
            bytes_accessed=extended.size * 4 + rows * cols * chans * 4,
        ),
    )(extended.astype(jnp.float32), kb)


def local_section(extended, raw, sigma, w_in, w_out):
    kernel = masked_kernel(raw, sigma)
    conv_out = depthwise(extended, kernel)
    field = extended[7 : extended.shape[0] - 7, 7 : extended.shape[1] - 7]
    mean = jnp.mean(conv_out, axis=-1, keepdims=True)
    var = jnp.mean((conv_out - mean) ** 2, axis=-1, keepdims=True)
    normed = ((conv_out - mean) * lax.rsqrt(var + 1e-06)).astype(jnp.bfloat16)
    hidden = jax.nn.gelu(jnp.dot(normed, w_in, preferred_element_type=jnp.float32)).astype(
        jnp.bfloat16
    )
    mixed = jnp.dot(hidden, w_out, preferred_element_type=jnp.float32)
    return (field.astype(jnp.float32) + mixed).astype(jnp.bfloat16)


def blur_down(padded):
    rows = padded.shape[0] - 2
    cols = padded.shape[1] - 2
    padded = padded.astype(jnp.float32)
    upper = padded[0:rows].reshape(rows // 2, 2, cols + 2, -1)
    lower = padded[2 : rows + 2].reshape(rows // 2, 2, cols + 2, -1)
    vert = (upper[:, 0] + 3.0 * upper[:, 1] + 3.0 * lower[:, 0] + lower[:, 1]) / 8.0
    left = vert[:, 0:cols].reshape(rows // 2, cols // 2, 2, -1)
    right = vert[:, 2 : cols + 2].reshape(rows // 2, cols // 2, 2, -1)
    return (
        (left[:, :, 0] + 3.0 * left[:, :, 1] + 3.0 * right[:, :, 0] + right[:, :, 1]) / 8.0
    ).astype(jnp.bfloat16)


def on_device(
    image,
    raw_first,
    sigma_first,
    in_first,
    out_first,
    widen,
    raw_second,
    sigma_second,
    in_second,
    out_second,
):
    reach = 7
    extended = padded_2(image, reach)
    first = local_section(extended, raw_first, sigma_first, in_first, out_first)
    first_cycle = padded_2(first, 1)
    first_pooled = blur_down(first_cycle)
    widened = jnp.dot(first_pooled, widen, preferred_element_type=jnp.float32).astype(jnp.bfloat16)
    widened_ext = padded_2(widened, reach)
    second = local_section(widened_ext, raw_second, sigma_second, in_second, out_second)
    second_cycle = padded_2(second, 1)
    return blur_down(second_cycle)


def solution(mesh):
    placed = (P("row", "col", None), P(), P(), P(), P(), P(), P(), P(), P(), P())
    return jax.shard_map(
        on_device, mesh=mesh, in_specs=placed, out_specs=P("row", "col", None), check_vma=False
    )
```

```python
import functools

import jax
import jax.numpy as jnp
from jax import lax
from jax.experimental import pallas as pl
from jax.experimental.pallas import tpu as pltpu
from jax.sharding import PartitionSpec as P


def padded_2(block, sides, width):
    for axis, dim in sides:
        count = lax.axis_size(axis)
        forward = [(i, i + 1) for i in range(count - 1)]
        backward = [(target, source) for source, target in forward]
        low = lax.ppermute(
            lax.slice_in_dim(block, block.shape[dim] - width, None, axis=dim), axis, forward
        )
        high = lax.ppermute(lax.slice_in_dim(block, 0, width, axis=dim), axis, backward)
        block = jnp.concatenate([low, block, high], axis=dim)
    return block


def masked_kernel(raw, sigma):
    offsets = jnp.arange(raw.shape[0]).astype(jnp.float32) - 7.0
    dist = offsets[:, None] ** 2 + offsets[None, :] ** 2
    mask = jnp.exp(-dist[:, :, None] / (2.0 * sigma[None, None, :] ** 2))
    return (raw * mask).astype(jnp.bfloat16)


def _dw_body(x_ref, k_ref, o_ref, xs_ref, *, taps, rows, cols, chans, rb):
    nlb = chans // 128
    njb = cols // 8
    nrb = rows // rb
    for b in range(taps):
        def shift(r, c):
            xs_ref[r] = x_ref[r, pl.ds(b, cols), :]
            return c

        lax.fori_loop(0, rows + taps - 1, shift, 0)
        for lb in range(nlb):
            lanes = pl.ds(lb * 128, 128)
            ks = [k_ref[a, b, :, lanes] for a in range(taps)]

            def body(i, c):
                r0 = pl.multiple_of((i // njb) * rb, rb)
                j0 = pl.multiple_of((i % njb) * 8, 8)
                xs = xs_ref[pl.ds(r0, rb + taps - 1), pl.ds(j0, 8), lanes]
                if b == 0:
                    acc = jnp.zeros((rb, 8, 128), jnp.float32)
                else:
                    acc = o_ref[pl.ds(r0, rb), pl.ds(j0, 8), lanes]
                terms = [xs[a : a + rb] * ks[a][None] for a in range(taps)]
                for g in range(0, taps, 5):
                    group = terms[g : g + 5]
                    while len(group) > 1:
                        group = [
                            group[i] + group[i + 1] if i + 1 < len(group) else group[i]
                            for i in range(0, len(group), 2)
                        ]
                    acc = acc + group[0]
                o_ref[pl.ds(r0, rb), pl.ds(j0, 8), lanes] = acc
                return c

            lax.fori_loop(0, nrb * njb, body, 0, unroll=2)


def depthwise(extended, kernel):
    taps = kernel.shape[0]
    rows = extended.shape[0] - taps + 1
    cols = extended.shape[1] - taps + 1
    chans = extended.shape[2]
    kb = jnp.broadcast_to(kernel.astype(jnp.float32)[:, :, None, :], (taps, taps, 8, chans))
    body = functools.partial(_dw_body, taps=taps, rows=rows, cols=cols, chans=chans, rb=8)
    vmem = pl.BlockSpec(memory_space=pltpu.VMEM)
    return pl.pallas_call(
        body,
        out_shape=jax.ShapeDtypeStruct((rows, cols, chans), jnp.float32),
        in_specs=[vmem, vmem],
        out_specs=vmem,
        scratch_shapes=[pltpu.VMEM((extended.shape[0], cols, chans), jnp.float32)],
        cost_estimate=pl.CostEstimate(
            flops=2 * rows * cols * chans * taps * taps,
            transcendentals=0,
            bytes_accessed=extended.size * 4 + rows * cols * chans * 4,
        ),
    )(extended.astype(jnp.float32), kb)


def local_section(extended, raw, sigma, w_in, w_out):
    kernel = masked_kernel(raw, sigma)
    conv_out = depthwise(extended, kernel)
    field = extended[7 : extended.shape[0] - 7, 7 : extended.shape[1] - 7]
    mean = jnp.mean(conv_out, axis=-1, keepdims=True)
    var = jnp.mean((conv_out - mean) ** 2, axis=-1, keepdims=True)
    normed = ((conv_out - mean) * lax.rsqrt(var + 1e-06)).astype(jnp.bfloat16)
    hidden = jax.nn.gelu(jnp.dot(normed, w_in, preferred_element_type=jnp.float32)).astype(
        jnp.bfloat16
    )
    mixed = jnp.dot(hidden, w_out, preferred_element_type=jnp.float32)
    return (field.astype(jnp.float32) + mixed).astype(jnp.bfloat16)


def blur_down(padded):
    rows = padded.shape[0] - 2
    cols = padded.shape[1] - 2
    padded = padded.astype(jnp.float32)
    upper = padded[0:rows].reshape(rows // 2, 2, cols + 2, -1)
    lower = padded[2 : rows + 2].reshape(rows // 2, 2, cols + 2, -1)
    vert = (upper[:, 0] + 3.0 * upper[:, 1] + 3.0 * lower[:, 0] + lower[:, 1]) / 8.0
    left = vert[:, 0:cols].reshape(rows // 2, cols // 2, 2, -1)
    right = vert[:, 2 : cols + 2].reshape(rows // 2, cols // 2, 2, -1)
    return (
        (left[:, :, 0] + 3.0 * left[:, :, 1] + 3.0 * right[:, :, 0] + right[:, :, 1]) / 8.0
    ).astype(jnp.bfloat16)


def on_device(
    image,
    raw_first,
    sigma_first,
    in_first,
    out_first,
    widen,
    raw_second,
    sigma_second,
    in_second,
    out_second,
):
    reach = 7
    extended = padded_2(image, (("row", 0), ("col", 1)), reach)
    first = local_section(extended, raw_first, sigma_first, in_first, out_first)
    first_cycle = padded_2(first, (("row", 0), ("col", 1)), 2 * reach + 1)
    first_pooled = zero_outside(blur_down(first_cycle), reach)
    widened_ext = jnp.dot(first_pooled, widen, preferred_element_type=jnp.float32).astype(
        jnp.bfloat16
    )
    second = local_section(widened_ext, raw_second, sigma_second, in_second, out_second)
    second_cycle = padded_2(second, (("row", 0), ("col", 1)), 1)
    return blur_down(second_cycle)


def zero_outside(block, width):
    keep = None
    for axis, dim in (("row", 0), ("col", 1)):
        index = lax.axis_index(axis)
        last = lax.axis_size(axis) - 1
        pos = lax.broadcasted_iota(jnp.int32, block.shape[:2], dim)
        ok = ((pos >= width) | (index != 0)) & ((pos < block.shape[dim] - width) | (index != last))
        keep = ok if keep is None else keep & ok
    return jnp.where(keep[:, :, None], block, jnp.zeros_like(block))


def solution(mesh):
    placed = (P("row", "col", None), P(), P(), P(), P(), P(), P(), P(), P(), P())
    return jax.shard_map(
        on_device, mesh=mesh, in_specs=placed, out_specs=P("row", "col", None), check_vma=False
    )
```

```python
import functools

import jax
import jax.numpy as jnp
from jax import lax
from jax.experimental import pallas as pl
from jax.experimental.pallas import tpu as pltpu
from jax.sharding import PartitionSpec as P


def padded_2(block, sides, width):
    for axis, dim in sides:
        count = lax.axis_size(axis)
        forward = [(i, i + 1) for i in range(count - 1)]
        backward = [(target, source) for source, target in forward]
        low = lax.ppermute(
            lax.slice_in_dim(block, block.shape[dim] - width, None, axis=dim), axis, forward
        )
        high = lax.ppermute(lax.slice_in_dim(block, 0, width, axis=dim), axis, backward)
        block = jnp.concatenate([low, block, high], axis=dim)
    return block


def masked_kernel(raw, sigma):
    offsets = jnp.arange(raw.shape[0]).astype(jnp.float32) - 7.0
    dist = offsets[:, None] ** 2 + offsets[None, :] ** 2
    mask = jnp.exp(-dist[:, :, None] / (2.0 * sigma[None, None, :] ** 2))
    return (raw * mask).astype(jnp.bfloat16)


def _dw_body(x_ref, k_ref, o_ref, xs_ref, *, taps, rows, cols, chans, rb):
    nlb = chans // 128
    njb = cols // 8
    nrb = rows // rb
    for b in range(taps):
        def shift(r, c):
            xs_ref[r] = x_ref[r, pl.ds(b, cols), :]
            return c

        lax.fori_loop(0, rows + taps - 1, shift, 0)
        for lb in range(nlb):
            lanes = pl.ds(lb * 128, 128)
            ks = [k_ref[a, b, :, lanes] for a in range(taps)]

            def body(i, c):
                r0 = pl.multiple_of((i // njb) * rb, rb)
                j0 = pl.multiple_of((i % njb) * 8, 8)
                xs = xs_ref[pl.ds(r0, rb + taps - 1), pl.ds(j0, 8), lanes]
                if b == 0:
                    acc = jnp.zeros((rb, 8, 128), jnp.float32)
                else:
                    acc = o_ref[pl.ds(r0, rb), pl.ds(j0, 8), lanes]
                terms = [xs[a : a + rb] * ks[a][None] for a in range(taps)]
                for g in range(0, taps, 5):
                    group = terms[g : g + 5]
                    while len(group) > 1:
                        group = [
                            group[i] + group[i + 1] if i + 1 < len(group) else group[i]
                            for i in range(0, len(group), 2)
                        ]
                    acc = acc + group[0]
                o_ref[pl.ds(r0, rb), pl.ds(j0, 8), lanes] = acc
                return c

            lax.fori_loop(0, nrb * njb, body, 0, unroll=2)


def depthwise(extended, kernel):
    taps = kernel.shape[0]
    rows = extended.shape[0] - taps + 1
    cols = extended.shape[1] - taps + 1
    chans = extended.shape[2]
    kb = jnp.broadcast_to(kernel.astype(jnp.float32)[:, :, None, :], (taps, taps, 8, chans))
    body = functools.partial(_dw_body, taps=taps, rows=rows, cols=cols, chans=chans, rb=8)
    vmem = pl.BlockSpec(memory_space=pltpu.VMEM)
    return pl.pallas_call(
        body,
        out_shape=jax.ShapeDtypeStruct((rows, cols, chans), jnp.float32),
        in_specs=[vmem, vmem],
        out_specs=vmem,
        scratch_shapes=[pltpu.VMEM((extended.shape[0], cols, chans), jnp.float32)],
        cost_estimate=pl.CostEstimate(
            flops=2 * rows * cols * chans * taps * taps,
            transcendentals=0,
            bytes_accessed=extended.size * 4 + rows * cols * chans * 4,
        ),
    )(extended.astype(jnp.float32), kb)


def local_section(extended, raw, sigma, w_in, w_out):
    kernel = masked_kernel(raw, sigma)
    conv_out = depthwise(extended, kernel)
    field = extended[7 : extended.shape[0] - 7, 7 : extended.shape[1] - 7]
    mean = jnp.mean(conv_out, axis=-1, keepdims=True)
    var = jnp.mean((conv_out - mean) ** 2, axis=-1, keepdims=True)
    normed = ((conv_out - mean) * lax.rsqrt(var + 1e-06)).astype(jnp.bfloat16)
    hidden = jax.nn.gelu(jnp.dot(normed, w_in, preferred_element_type=jnp.float32)).astype(
        jnp.bfloat16
    )
    mixed = jnp.dot(hidden, w_out, preferred_element_type=jnp.float32)
    return (field.astype(jnp.float32) + mixed).astype(jnp.bfloat16)


def blur_down(padded):
    rows = padded.shape[0] - 2
    cols = padded.shape[1] - 2
    padded = padded.astype(jnp.float32)
    upper = padded[0:rows].reshape(rows // 2, 2, cols + 2, -1)
    lower = padded[2 : rows + 2].reshape(rows // 2, 2, cols + 2, -1)
    vert = (upper[:, 0] + 3.0 * upper[:, 1] + 3.0 * lower[:, 0] + lower[:, 1]) / 8.0
    left = vert[:, 0:cols].reshape(rows // 2, cols // 2, 2, -1)
    right = vert[:, 2 : cols + 2].reshape(rows // 2, cols // 2, 2, -1)
    return (
        (left[:, :, 0] + 3.0 * left[:, :, 1] + 3.0 * right[:, :, 0] + right[:, :, 1]) / 8.0
    ).astype(jnp.bfloat16)


def on_device(
    image,
    raw_first,
    sigma_first,
    in_first,
    out_first,
    widen,
    raw_second,
    sigma_second,
    in_second,
    out_second,
):
    reach = 7
    extended = padded_2(image, (("row", 0), ("col", 1)), reach)
    first = local_section(extended, raw_first, sigma_first, in_first, out_first)
    first_cycle = padded_2(first, (("row", 0), ("col", 1)), 2 * reach + 3)
    first_pooled = zero_outside(blur_down(first_cycle), reach + 1)
    widened_ext = jnp.dot(first_pooled, widen, preferred_element_type=jnp.float32).astype(
        jnp.bfloat16
    )[1:-1, 1:-1]
    second = local_section(widened_ext, raw_second, sigma_second, in_second, out_second)
    second_cycle = padded_2(second, (("row", 0), ("col", 1)), 1)
    return blur_down(second_cycle)


def zero_outside(block, width):
    keep = None
    for axis, dim in (("row", 0), ("col", 1)):
        index = lax.axis_index(axis)
        last = lax.axis_size(axis) - 1
        pos = lax.broadcasted_iota(jnp.int32, block.shape[:2], dim)
        ok = ((pos >= width) | (index != 0)) & ((pos < block.shape[dim] - width) | (index != last))
        keep = ok if keep is None else keep & ok
    return jnp.where(keep[:, :, None], block, jnp.zeros_like(block))


def solution(mesh):
    placed = (P("row", "col", None), P(), P(), P(), P(), P(), P(), P(), P(), P())
    return jax.shard_map(
        on_device, mesh=mesh, in_specs=placed, out_specs=P("row", "col", None), check_vma=False
    )
```

```python
import functools

import jax
import jax.numpy as jnp
from jax import lax
from jax.experimental import pallas as pl
from jax.experimental.pallas import tpu as pltpu
from jax.sharding import PartitionSpec as P


def padded_2(block, sides, width):
    for axis, dim in sides:
        count = lax.axis_size(axis)
        forward = [(i, i + 1) for i in range(count - 1)]
        backward = [(target, source) for source, target in forward]
        low = lax.ppermute(
            lax.slice_in_dim(block, block.shape[dim] - width, None, axis=dim), axis, forward
        )
        high = lax.ppermute(lax.slice_in_dim(block, 0, width, axis=dim), axis, backward)
        block = jnp.concatenate([low, block, high], axis=dim)
    return block


def masked_kernel(raw, sigma):
    offsets = jnp.arange(raw.shape[0]).astype(jnp.float32) - 7.0
    dist = offsets[:, None] ** 2 + offsets[None, :] ** 2
    mask = jnp.exp(-dist[:, :, None] / (2.0 * sigma[None, None, :] ** 2))
    return (raw * mask).astype(jnp.bfloat16)


def _dw_body(x_ref, k_ref, o_ref, xs_ref, *, taps, rows, cols, chans, rb):
    nlb = chans // 128
    njb = cols // 8
    nrb = rows // rb
    first = True
    for s in range(8):
        if s == 0:
            src = x_ref
        else:
            width = cols + 8 if s + 8 < taps else cols

            def shift(r, c):
                xs_ref[r, pl.ds(0, width), :] = x_ref[r, pl.ds(s, width), :]
                return c

            lax.fori_loop(0, rows + taps - 1, shift, 0)
            src = xs_ref
        for q in range(2):
            b = 8 * q + s
            if b >= taps:
                continue
            for lb in range(nlb):
                lanes = pl.ds(lb * 128, 128)
                ks = [k_ref[a, b, :, lanes] for a in range(taps)]

                def body(i, c, src=src, q=q, ks=ks, lanes=lanes, first=first):
                    r0 = pl.multiple_of((i // njb) * rb, rb)
                    j0 = pl.multiple_of((i % njb) * 8, 8)
                    xs = src[pl.ds(r0, rb + taps - 1), pl.ds(j0 + 8 * q, 8), lanes]
                    if first:
                        acc = jnp.zeros((rb, 8, 128), jnp.float32)
                    else:
                        acc = o_ref[pl.ds(r0, rb), pl.ds(j0, 8), lanes]
                    terms = [xs[a : a + rb] * ks[a][None] for a in range(taps)]
                    for g in range(0, taps, 5):
                        group = terms[g : g + 5]
                        while len(group) > 1:
                            group = [
                                group[i] + group[i + 1] if i + 1 < len(group) else group[i]
                                for i in range(0, len(group), 2)
                            ]
                        acc = acc + group[0]
                    o_ref[pl.ds(r0, rb), pl.ds(j0, 8), lanes] = acc
                    return c

                lax.fori_loop(0, nrb * njb, body, 0, unroll=2)
            first = False


def depthwise(extended, kernel):
    taps = kernel.shape[0]
    rows = extended.shape[0] - taps + 1
    cols = extended.shape[1] - taps + 1
    chans = extended.shape[2]
    kb = jnp.broadcast_to(kernel.astype(jnp.float32)[:, :, None, :], (taps, taps, 8, chans))
    body = functools.partial(_dw_body, taps=taps, rows=rows, cols=cols, chans=chans, rb=8)
    vmem = pl.BlockSpec(memory_space=pltpu.VMEM)
    return pl.pallas_call(
        body,
        out_shape=jax.ShapeDtypeStruct((rows, cols, chans), jnp.float32),
        in_specs=[vmem, vmem],
        out_specs=vmem,
        scratch_shapes=[pltpu.VMEM((extended.shape[0], cols + 8, chans), jnp.float32)],
        cost_estimate=pl.CostEstimate(
            flops=2 * rows * cols * chans * taps * taps,
            transcendentals=0,
            bytes_accessed=extended.size * 4 + rows * cols * chans * 4,
        ),
    )(extended.astype(jnp.float32), kb)


def local_section(extended, raw, sigma, w_in, w_out):
    kernel = masked_kernel(raw, sigma)
    conv_out = depthwise(extended, kernel)
    field = extended[7 : extended.shape[0] - 7, 7 : extended.shape[1] - 7]
    mean = jnp.mean(conv_out, axis=-1, keepdims=True)
    var = jnp.mean((conv_out - mean) ** 2, axis=-1, keepdims=True)
    normed = ((conv_out - mean) * lax.rsqrt(var + 1e-06)).astype(jnp.bfloat16)
    hidden = jax.nn.gelu(jnp.dot(normed, w_in, preferred_element_type=jnp.float32)).astype(
        jnp.bfloat16
    )
    mixed = jnp.dot(hidden, w_out, preferred_element_type=jnp.float32)
    return (field.astype(jnp.float32) + mixed).astype(jnp.bfloat16)


def blur_down(padded):
    rows = padded.shape[0] - 2
    cols = padded.shape[1] - 2
    padded = padded.astype(jnp.float32)
    upper = padded[0:rows].reshape(rows // 2, 2, cols + 2, -1)
    lower = padded[2 : rows + 2].reshape(rows // 2, 2, cols + 2, -1)
    vert = (upper[:, 0] + 3.0 * upper[:, 1] + 3.0 * lower[:, 0] + lower[:, 1]) / 8.0
    left = vert[:, 0:cols].reshape(rows // 2, cols // 2, 2, -1)
    right = vert[:, 2 : cols + 2].reshape(rows // 2, cols // 2, 2, -1)
    return (
        (left[:, :, 0] + 3.0 * left[:, :, 1] + 3.0 * right[:, :, 0] + right[:, :, 1]) / 8.0
    ).astype(jnp.bfloat16)


def on_device(
    image,
    raw_first,
    sigma_first,
    in_first,
    out_first,
    widen,
    raw_second,
    sigma_second,
    in_second,
    out_second,
):
    reach = 7
    extended = padded_2(image, (("row", 0), ("col", 1)), reach)
    first = local_section(extended, raw_first, sigma_first, in_first, out_first)
    first_cycle = padded_2(first, (("row", 0), ("col", 1)), 1)
    first_pooled = blur_down(first_cycle)
    widened = jnp.dot(first_pooled, widen, preferred_element_type=jnp.float32).astype(jnp.bfloat16)
    widened_ext = padded_2(widened, (("row", 0), ("col", 1)), reach)
    second = local_section(widened_ext, raw_second, sigma_second, in_second, out_second)
    second_cycle = padded_2(second, (("row", 0), ("col", 1)), 1)
    return blur_down(second_cycle)


def solution(mesh):
    placed = (P("row", "col", None), P(), P(), P(), P(), P(), P(), P(), P(), P())
    return jax.shard_map(
        on_device, mesh=mesh, in_specs=placed, out_specs=P("row", "col", None), check_vma=False
    )
```

```python
import functools

import jax
import jax.numpy as jnp
from jax import lax
from jax.experimental import pallas as pl
from jax.experimental.pallas import tpu as pltpu
from jax.sharding import PartitionSpec as P


def padded_2(block, sides, width):
    for axis, dim in sides:
        count = lax.axis_size(axis)
        forward = [(i, i + 1) for i in range(count - 1)]
        backward = [(target, source) for source, target in forward]
        low = lax.ppermute(
            lax.slice_in_dim(block, block.shape[dim] - width, None, axis=dim), axis, forward
        )
        high = lax.ppermute(lax.slice_in_dim(block, 0, width, axis=dim), axis, backward)
        block = jnp.concatenate([low, block, high], axis=dim)
    return block


def masked_kernel(raw, sigma):
    offsets = jnp.arange(raw.shape[0]).astype(jnp.float32) - 7.0
    dist = offsets[:, None] ** 2 + offsets[None, :] ** 2
    mask = jnp.exp(-dist[:, :, None] / (2.0 * sigma[None, None, :] ** 2))
    return (raw * mask).astype(jnp.bfloat16)


def _dw_body(x_ref, k_ref, w_in_ref, w_out_ref, y_ref, o_ref, xs_ref, *, taps, rows, cols, chans, rb):
    nlb = chans // 128
    njb = cols // 8
    nrb = rows // rb
    first = True
    for s in range(8):
        if s == 0:
            src = x_ref
        else:
            width = cols + 8 if s + 8 < taps else cols

            def shift(r, c):
                xs_ref[r, pl.ds(0, width), :] = x_ref[r, pl.ds(s, width), :]
                return c

            lax.fori_loop(0, rows + taps - 1, shift, 0)
            src = xs_ref
        for q in range(2):
            b = 8 * q + s
            if b >= taps:
                continue
            for lb in range(nlb):
                lanes = pl.ds(lb * 128, 128)
                ks = [k_ref[a, b, :, lanes] for a in range(taps)]

                def body(i, c, src=src, q=q, ks=ks, lanes=lanes, first=first):
                    r0 = pl.multiple_of((i // njb) * rb, rb)
                    j0 = pl.multiple_of((i % njb) * 8, 8)
                    xs = src[pl.ds(r0, rb + taps - 1), pl.ds(j0 + 8 * q, 8), lanes]
                    if first:
                        acc = jnp.zeros((rb, 8, 128), jnp.float32)
                    else:
                        acc = o_ref[pl.ds(r0, rb), pl.ds(j0, 8), lanes]
                    terms = [xs[a : a + rb] * ks[a][None] for a in range(taps)]
                    for g in range(0, taps, 5):
                        group = terms[g : g + 5]
                        while len(group) > 1:
                            group = [
                                group[i] + group[i + 1] if i + 1 < len(group) else group[i]
                                for i in range(0, len(group), 2)
                            ]
                        acc = acc + group[0]
                    o_ref[pl.ds(r0, rb), pl.ds(j0, 8), lanes] = acc
                    return c

                lax.fori_loop(0, nrb * njb, body, 0, unroll=2)
            first = False

    er = 2
    half = (taps - 1) // 2

    def epilogue(i, c):
        r0 = pl.multiple_of(i * er, er)
        d = o_ref[pl.ds(r0, er)].reshape(er * cols, chans)
        mean = jnp.mean(d, axis=-1, keepdims=True)
        var = jnp.mean((d - mean) ** 2, axis=-1, keepdims=True)
        normed = ((d - mean) * lax.rsqrt(var + 1e-06)).astype(jnp.bfloat16)
        hidden = jnp.dot(normed, w_in_ref[...], preferred_element_type=jnp.float32)
        hidden = jax.nn.gelu(hidden).astype(jnp.bfloat16)
        mixed = jnp.dot(hidden, w_out_ref[...], preferred_element_type=jnp.float32)
        field = x_ref[pl.ds(r0 + half, er), pl.ds(half, cols), :].reshape(er * cols, chans)
        y_ref[pl.ds(r0, er)] = (field + mixed).astype(y_ref.dtype).reshape(er, cols, chans)
        return c

    lax.fori_loop(0, rows // er, epilogue, 0)


def local_section(extended, raw, sigma, w_in, w_out):
    kernel = masked_kernel(raw, sigma)
    taps = kernel.shape[0]
    rows = extended.shape[0] - taps + 1
    cols = extended.shape[1] - taps + 1
    chans = extended.shape[2]
    hid = w_in.shape[1]
    kb = jnp.broadcast_to(kernel.astype(jnp.float32)[:, :, None, :], (taps, taps, 8, chans))
    body = functools.partial(_dw_body, taps=taps, rows=rows, cols=cols, chans=chans, rb=8)
    vmem = pl.BlockSpec(memory_space=pltpu.VMEM)
    return pl.pallas_call(
        body,
        out_shape=jax.ShapeDtypeStruct((rows, cols, chans), jnp.bfloat16),
        in_specs=[vmem, vmem, vmem, vmem],
        out_specs=vmem,
        scratch_shapes=[
            pltpu.VMEM((rows, cols, chans), jnp.float32),
            pltpu.VMEM((extended.shape[0], cols + 8, chans), jnp.float32),
        ],
        cost_estimate=pl.CostEstimate(
            flops=2 * rows * cols * chans * (taps * taps + 2 * hid),
            transcendentals=rows * cols * hid,
            bytes_accessed=extended.size * 4 + rows * cols * chans * 2,
        ),
    )(extended.astype(jnp.float32), kb, w_in, w_out)


def blur_down(padded):
    rows = padded.shape[0] - 2
    cols = padded.shape[1] - 2
    padded = padded.astype(jnp.float32)
    upper = padded[0:rows].reshape(rows // 2, 2, cols + 2, -1)
    lower = padded[2 : rows + 2].reshape(rows // 2, 2, cols + 2, -1)
    vert = (upper[:, 0] + 3.0 * upper[:, 1] + 3.0 * lower[:, 0] + lower[:, 1]) / 8.0
    left = vert[:, 0:cols].reshape(rows // 2, cols // 2, 2, -1)
    right = vert[:, 2 : cols + 2].reshape(rows // 2, cols // 2, 2, -1)
    return (
        (left[:, :, 0] + 3.0 * left[:, :, 1] + 3.0 * right[:, :, 0] + right[:, :, 1]) / 8.0
    ).astype(jnp.bfloat16)


def on_device(
    image,
    raw_first,
    sigma_first,
    in_first,
    out_first,
    widen,
    raw_second,
    sigma_second,
    in_second,
    out_second,
):
    reach = 7
    extended = padded_2(image, (("row", 0), ("col", 1)), reach)
    first = local_section(extended, raw_first, sigma_first, in_first, out_first)
    first_cycle = padded_2(first, (("row", 0), ("col", 1)), 1)
    first_pooled = blur_down(first_cycle)
    widened = jnp.dot(first_pooled, widen, preferred_element_type=jnp.float32).astype(jnp.bfloat16)
    widened_ext = padded_2(widened, (("row", 0), ("col", 1)), reach)
    second = local_section(widened_ext, raw_second, sigma_second, in_second, out_second)
    second_cycle = padded_2(second, (("row", 0), ("col", 1)), 1)
    return blur_down(second_cycle)


def solution(mesh):
    placed = (P("row", "col", None), P(), P(), P(), P(), P(), P(), P(), P(), P())
    return jax.shard_map(
        on_device, mesh=mesh, in_specs=placed, out_specs=P("row", "col", None), check_vma=False
    )
```

```python
import functools

import jax
import jax.numpy as jnp
from jax import lax
from jax.experimental import pallas as pl
from jax.experimental.pallas import tpu as pltpu
from jax.sharding import PartitionSpec as P


def padded_2(block, sides, width):
    for axis, dim in sides:
        count = lax.axis_size(axis)
        forward = [(i, i + 1) for i in range(count - 1)]
        backward = [(target, source) for source, target in forward]
        low = lax.ppermute(
            lax.slice_in_dim(block, block.shape[dim] - width, None, axis=dim), axis, forward
        )
        high = lax.ppermute(lax.slice_in_dim(block, 0, width, axis=dim), axis, backward)
        block = jnp.concatenate([low, block, high], axis=dim)
    return block


def masked_kernel(raw, sigma):
    offsets = jnp.arange(raw.shape[0]).astype(jnp.float32) - 7.0
    dist = offsets[:, None] ** 2 + offsets[None, :] ** 2
    mask = jnp.exp(-dist[:, :, None] / (2.0 * sigma[None, None, :] ** 2))
    return (raw * mask).astype(jnp.bfloat16)


def _dw_body(x_ref, k_ref, o_ref, xf_ref, xs_ref, *, taps, rows, cols, chans, rb):
    nlb = chans // 128
    njb = cols // 8
    nrb = rows // rb

    def widen_row(r, c):
        xf_ref[r] = x_ref[r].astype(jnp.float32)
        return c

    lax.fori_loop(0, rows + taps - 1, widen_row, 0)
    first = True
    for s in range(8):
        if s == 0:
            src = xf_ref
        else:
            width = cols + 8 if s + 8 < taps else cols

            def shift(r, c):
                xs_ref[r, pl.ds(0, width), :] = xf_ref[r, pl.ds(s, width), :]
                return c

            lax.fori_loop(0, rows + taps - 1, shift, 0)
            src = xs_ref
        for q in range(2):
            b = 8 * q + s
            if b >= taps:
                continue
            for lb in range(nlb):
                lanes = pl.ds(lb * 128, 128)
                ks = [jnp.broadcast_to(k_ref[a, pl.ds(b, 1), lanes], (8, 128)) for a in range(taps)]

                def body(i, c, src=src, q=q, ks=ks, lanes=lanes, first=first):
                    r0 = pl.multiple_of((i // njb) * rb, rb)
                    j0 = pl.multiple_of((i % njb) * 8, 8)
                    xs = src[pl.ds(r0, rb + taps - 1), pl.ds(j0 + 8 * q, 8), lanes]
                    if first:
                        acc = jnp.zeros((rb, 8, 128), jnp.float32)
                    else:
                        acc = o_ref[pl.ds(r0, rb), pl.ds(j0, 8), lanes]
                    terms = [xs[a : a + rb] * ks[a][None] for a in range(taps)]
                    for g in range(0, taps, 5):
                        group = terms[g : g + 5]
                        while len(group) > 1:
                            group = [
                                group[i] + group[i + 1] if i + 1 < len(group) else group[i]
                                for i in range(0, len(group), 2)
                            ]
                        acc = acc + group[0]
                    o_ref[pl.ds(r0, rb), pl.ds(j0, 8), lanes] = acc
                    return c

                lax.fori_loop(0, nrb * njb, body, 0, unroll=2)
            first = False


def depthwise(extended, kernel):
    taps = kernel.shape[0]
    rows = extended.shape[0] - taps + 1
    cols = extended.shape[1] - taps + 1
    chans = extended.shape[2]
    body = functools.partial(_dw_body, taps=taps, rows=rows, cols=cols, chans=chans, rb=8)
    vmem = pl.BlockSpec(memory_space=pltpu.VMEM)
    return pl.pallas_call(
        body,
        out_shape=jax.ShapeDtypeStruct((rows, cols, chans), jnp.float32),
        in_specs=[vmem, vmem],
        out_specs=vmem,
        scratch_shapes=[
            pltpu.VMEM(extended.shape, jnp.float32),
            pltpu.VMEM((extended.shape[0], cols + 8, chans), jnp.float32),
        ],
        cost_estimate=pl.CostEstimate(
            flops=2 * rows * cols * chans * taps * taps,
            transcendentals=0,
            bytes_accessed=extended.size * 2 + rows * cols * chans * 4,
        ),
    )(extended, kernel.astype(jnp.float32))


def local_section(extended, raw, sigma, w_in, w_out):
    kernel = masked_kernel(raw, sigma)
    conv_out = depthwise(extended, kernel)
    field = extended[7 : extended.shape[0] - 7, 7 : extended.shape[1] - 7]
    mean = jnp.mean(conv_out, axis=-1, keepdims=True)
    var = jnp.mean((conv_out - mean) ** 2, axis=-1, keepdims=True)
    normed = ((conv_out - mean) * lax.rsqrt(var + 1e-06)).astype(jnp.bfloat16)
    hidden = jax.nn.gelu(jnp.dot(normed, w_in, preferred_element_type=jnp.float32)).astype(
        jnp.bfloat16
    )
    mixed = jnp.dot(hidden, w_out, preferred_element_type=jnp.float32)
    return (field.astype(jnp.float32) + mixed).astype(jnp.bfloat16)


def blur_down(padded):
    rows = padded.shape[0] - 2
    cols = padded.shape[1] - 2
    padded = padded.astype(jnp.float32)
    upper = padded[0:rows].reshape(rows // 2, 2, cols + 2, -1)
    lower = padded[2 : rows + 2].reshape(rows // 2, 2, cols + 2, -1)
    vert = (upper[:, 0] + 3.0 * upper[:, 1] + 3.0 * lower[:, 0] + lower[:, 1]) / 8.0
    left = vert[:, 0:cols].reshape(rows // 2, cols // 2, 2, -1)
    right = vert[:, 2 : cols + 2].reshape(rows // 2, cols // 2, 2, -1)
    return (
        (left[:, :, 0] + 3.0 * left[:, :, 1] + 3.0 * right[:, :, 0] + right[:, :, 1]) / 8.0
    ).astype(jnp.bfloat16)


def on_device(
    image,
    raw_first,
    sigma_first,
    in_first,
    out_first,
    widen,
    raw_second,
    sigma_second,
    in_second,
    out_second,
):
    reach = 7
    extended = padded_2(image, (("row", 0), ("col", 1)), reach)
    first = local_section(extended, raw_first, sigma_first, in_first, out_first)
    first_cycle = padded_2(first, (("row", 0), ("col", 1)), 1)
    first_pooled = blur_down(first_cycle)
    widened = jnp.dot(first_pooled, widen, preferred_element_type=jnp.float32).astype(jnp.bfloat16)
    widened_ext = padded_2(widened, (("row", 0), ("col", 1)), reach)
    second = local_section(widened_ext, raw_second, sigma_second, in_second, out_second)
    second_cycle = padded_2(second, (("row", 0), ("col", 1)), 1)
    return blur_down(second_cycle)


def solution(mesh):
    placed = (P("row", "col", None), P(), P(), P(), P(), P(), P(), P(), P(), P())
    return jax.shard_map(
        on_device, mesh=mesh, in_specs=placed, out_specs=P("row", "col", None), check_vma=False
    )
```

```python
import functools

import jax
import jax.numpy as jnp
from jax import lax
from jax.experimental import pallas as pl
from jax.experimental.pallas import tpu as pltpu
from jax.sharding import PartitionSpec as P


def padded_2(block, sides, width):
    for axis, dim in sides:
        count = lax.axis_size(axis)
        forward = [(i, i + 1) for i in range(count - 1)]
        backward = [(target, source) for source, target in forward]
        low = lax.ppermute(
            lax.slice_in_dim(block, block.shape[dim] - width, None, axis=dim), axis, forward
        )
        high = lax.ppermute(lax.slice_in_dim(block, 0, width, axis=dim), axis, backward)
        block = jnp.concatenate([low, block, high], axis=dim)
    return block


def masked_kernel(raw, sigma):
    offsets = jnp.arange(raw.shape[0]).astype(jnp.float32) - 7.0
    dist = offsets[:, None] ** 2 + offsets[None, :] ** 2
    mask = jnp.exp(-dist[:, :, None] / (2.0 * sigma[None, None, :] ** 2))
    return (raw * mask).astype(jnp.bfloat16)


def _dw_body(x_all, k_ref, o_all, xf_ref, xs_ref, *, taps, base, rows, cols, chans, rb):
    nlb = chans // 128
    njb = cols // 8
    nrb = rows // rb

    def one_strip(n, carry):
        x_ref = x_all.at[n]
        o_ref = o_all.at[n]

        def widen_row(r, c):
            xf_ref[r] = x_ref[base + r].astype(jnp.float32)
            return c

        lax.fori_loop(0, rows + taps - 1, widen_row, 0)
        first = True
        for s in range(8):
            if s == 0:
                src = xf_ref
            else:
                width = cols + 8 if s + 8 < taps else cols

                def shift(r, c, s=s, width=width):
                    xs_ref[r, pl.ds(0, width), :] = xf_ref[r, pl.ds(s, width), :]
                    return c

                lax.fori_loop(0, rows + taps - 1, shift, 0)
                src = xs_ref
            for q in range(2):
                b = 8 * q + s
                if b >= taps:
                    continue
                for lb in range(nlb):
                    lanes = pl.ds(lb * 128, 128)
                    ks = [
                        jnp.broadcast_to(k_ref[a, pl.ds(b, 1), lanes], (8, 128))
                        for a in range(taps)
                    ]

                    def body(i, c, src=src, q=q, ks=ks, lanes=lanes, first=first):
                        r0 = pl.multiple_of((i // njb) * rb, rb)
                        j0 = pl.multiple_of((i % njb) * 8, 8)
                        xs = src[pl.ds(r0, rb + taps - 1), pl.ds(j0 + 8 * q, 8), lanes]
                        if first:
                            acc = jnp.zeros((rb, 8, 128), jnp.float32)
                        else:
                            acc = o_ref[pl.ds(r0, rb), pl.ds(j0, 8), lanes]
                        terms = [xs[a : a + rb] * ks[a][None] for a in range(taps)]
                        for g in range(0, taps, 5):
                            group = terms[g : g + 5]
                            while len(group) > 1:
                                group = [
                                    group[i] + group[i + 1] if i + 1 < len(group) else group[i]
                                    for i in range(0, len(group), 2)
                                ]
                            acc = acc + group[0]
                        o_ref[pl.ds(r0, rb), pl.ds(j0, 8), lanes] = acc
                        return c

                    lax.fori_loop(0, nrb * njb, body, 0, unroll=2)
                first = False
        return carry

    lax.fori_loop(0, x_all.shape[0], one_strip, 0)


def depthwise(strips, kernel, base, rows):
    taps = kernel.shape[0]
    count = strips.shape[0]
    cols = strips.shape[2] - taps + 1
    chans = strips.shape[3]
    body = functools.partial(
        _dw_body, taps=taps, base=base, rows=rows, cols=cols, chans=chans, rb=8
    )
    vmem = pl.BlockSpec(memory_space=pltpu.VMEM)
    return pl.pallas_call(
        body,
        out_shape=jax.ShapeDtypeStruct((count, rows, cols, chans), jnp.float32),
        in_specs=[vmem, vmem],
        out_specs=vmem,
        scratch_shapes=[
            pltpu.VMEM((rows + taps - 1,) + strips.shape[2:], jnp.float32),
            pltpu.VMEM((rows + taps - 1, cols + 8, chans), jnp.float32),
        ],
        cost_estimate=pl.CostEstimate(
            flops=2 * count * rows * cols * chans * taps * taps,
            transcendentals=0,
            bytes_accessed=strips.size * 2 + count * rows * cols * chans * 4,
        ),
    )(strips, kernel.astype(jnp.float32))


def exchange(block, axis, dim, width):
    count = lax.axis_size(axis)
    forward = [(i, i + 1) for i in range(count - 1)]
    backward = [(target, source) for source, target in forward]
    low = lax.ppermute(
        lax.slice_in_dim(block, block.shape[dim] - width, None, axis=dim), axis, forward
    )
    high = lax.ppermute(lax.slice_in_dim(block, 0, width, axis=dim), axis, backward)
    return jnp.concatenate([low, block, high], axis=dim)


def section_conv(block, kernel):
    reach = (kernel.shape[0] - 1) // 2
    rows = block.shape[0]
    band = 8
    wide = exchange(block, "col", 1, reach)
    middle = depthwise(wide[None], kernel, band - reach, rows - 2 * band)
    full = exchange(wide, "row", 0, reach)
    ends = jnp.stack(
        [full[: band + 2 * reach], full[rows - band :]], axis=0
    )
    edge = depthwise(ends, kernel, 0, band)
    return jnp.concatenate([edge[0], middle[0], edge[1]], axis=0)


def local_section(field, raw, sigma, w_in, w_out):
    kernel = masked_kernel(raw, sigma)
    conv_out = section_conv(field, kernel)
    mean = jnp.mean(conv_out, axis=-1, keepdims=True)
    var = jnp.mean((conv_out - mean) ** 2, axis=-1, keepdims=True)
    normed = ((conv_out - mean) * lax.rsqrt(var + 1e-06)).astype(jnp.bfloat16)
    hidden = jax.nn.gelu(jnp.dot(normed, w_in, preferred_element_type=jnp.float32)).astype(
        jnp.bfloat16
    )
    mixed = jnp.dot(hidden, w_out, preferred_element_type=jnp.float32)
    return (field.astype(jnp.float32) + mixed).astype(jnp.bfloat16)


def blur_down(padded):
    rows = padded.shape[0] - 2
    cols = padded.shape[1] - 2
    padded = padded.astype(jnp.float32)
    upper = padded[0:rows].reshape(rows // 2, 2, cols + 2, -1)
    lower = padded[2 : rows + 2].reshape(rows // 2, 2, cols + 2, -1)
    vert = (upper[:, 0] + 3.0 * upper[:, 1] + 3.0 * lower[:, 0] + lower[:, 1]) / 8.0
    left = vert[:, 0:cols].reshape(rows // 2, cols // 2, 2, -1)
    right = vert[:, 2 : cols + 2].reshape(rows // 2, cols // 2, 2, -1)
    return (
        (left[:, :, 0] + 3.0 * left[:, :, 1] + 3.0 * right[:, :, 0] + right[:, :, 1]) / 8.0
    ).astype(jnp.bfloat16)


def on_device(
    image,
    raw_first,
    sigma_first,
    in_first,
    out_first,
    widen,
    raw_second,
    sigma_second,
    in_second,
    out_second,
):
    first = local_section(image, raw_first, sigma_first, in_first, out_first)
    first_cycle = padded_2(first, (("row", 0), ("col", 1)), 1)
    first_pooled = blur_down(first_cycle)
    widened = jnp.dot(first_pooled, widen, preferred_element_type=jnp.float32).astype(jnp.bfloat16)
    second = local_section(widened, raw_second, sigma_second, in_second, out_second)
    second_cycle = padded_2(second, (("row", 0), ("col", 1)), 1)
    return blur_down(second_cycle)


def solution(mesh):
    placed = (P("row", "col", None), P(), P(), P(), P(), P(), P(), P(), P(), P())
    return jax.shard_map(
        on_device, mesh=mesh, in_specs=placed, out_specs=P("row", "col", None), check_vma=False
    )
```

```python
import functools

import jax
import jax.numpy as jnp
from jax import lax
from jax.experimental import pallas as pl
from jax.experimental.pallas import tpu as pltpu
from jax.sharding import PartitionSpec as P


def padded_2(block, sides, width):
    for axis, dim in sides:
        count = lax.axis_size(axis)
        forward = [(i, i + 1) for i in range(count - 1)]
        backward = [(target, source) for source, target in forward]
        low = lax.ppermute(
            lax.slice_in_dim(block, block.shape[dim] - width, None, axis=dim), axis, forward
        )
        high = lax.ppermute(lax.slice_in_dim(block, 0, width, axis=dim), axis, backward)
        block = jnp.concatenate([low, block, high], axis=dim)
    return block


def masked_kernel(raw, sigma):
    offsets = jnp.arange(raw.shape[0]).astype(jnp.float32) - 7.0
    dist = offsets[:, None] ** 2 + offsets[None, :] ** 2
    mask = jnp.exp(-dist[:, :, None] / (2.0 * sigma[None, None, :] ** 2))
    return (raw * mask).astype(jnp.bfloat16)


def _dw_body(x_all, k_ref, o_all, xf_ref, xs_ref, *, taps, cbase, rows, cols, chans, rb):
    nlb = chans // 128
    njb = cols // 8
    nrb = rows // rb

    def one_strip(n, carry):
        x_ref = x_all.at[n]
        o_ref = o_all.at[n]

        def widen_row(r, c):
            xf_ref[r] = x_ref[r].astype(jnp.float32)
            return c

        lax.fori_loop(0, rows + taps - 1, widen_row, 0)
        first = True
        for s in range(8):
            if cbase + s == 0:
                src = xf_ref
            else:
                width = cols + 8 if s + 8 < taps else cols

                def shift(r, c, s=s, width=width):
                    xs_ref[r, pl.ds(0, width), :] = xf_ref[r, pl.ds(cbase + s, width), :]
                    return c

                lax.fori_loop(0, rows + taps - 1, shift, 0)
                src = xs_ref
            for q in range(2):
                b = 8 * q + s
                if b >= taps:
                    continue
                for lb in range(nlb):
                    lanes = pl.ds(lb * 128, 128)
                    ks = [
                        jnp.broadcast_to(k_ref[a, pl.ds(b, 1), lanes], (8, 128))
                        for a in range(taps)
                    ]

                    def body(i, c, src=src, q=q, ks=ks, lanes=lanes, first=first):
                        r0 = pl.multiple_of((i // njb) * rb, rb)
                        j0 = pl.multiple_of((i % njb) * 8, 8)
                        xs = src[pl.ds(r0, rb + taps - 1), pl.ds(j0 + 8 * q, 8), lanes]
                        if first:
                            acc = jnp.zeros((rb, 8, 128), jnp.float32)
                        else:
                            acc = o_ref[pl.ds(r0, rb), pl.ds(j0, 8), lanes]
                        terms = [xs[a : a + rb] * ks[a][None] for a in range(taps)]
                        for g in range(0, taps, 5):
                            group = terms[g : g + 5]
                            while len(group) > 1:
                                group = [
                                    group[i] + group[i + 1] if i + 1 < len(group) else group[i]
                                    for i in range(0, len(group), 2)
                                ]
                            acc = acc + group[0]
                        o_ref[pl.ds(r0, rb), pl.ds(j0, 8), lanes] = acc
                        return c

                    lax.fori_loop(0, nrb * njb, body, 0, unroll=2)
                first = False
        return carry

    lax.fori_loop(0, x_all.shape[0], one_strip, 0)


def depthwise(strips, kernel, cbase, cols):
    taps = kernel.shape[0]
    count = strips.shape[0]
    rows = strips.shape[1] - taps + 1
    chans = strips.shape[3]
    body = functools.partial(
        _dw_body, taps=taps, cbase=cbase, rows=rows, cols=cols, chans=chans, rb=8
    )
    vmem = pl.BlockSpec(memory_space=pltpu.VMEM)
    return pl.pallas_call(
        body,
        out_shape=jax.ShapeDtypeStruct((count, rows, cols, chans), jnp.float32),
        in_specs=[vmem, vmem],
        out_specs=vmem,
        scratch_shapes=[
            pltpu.VMEM(strips.shape[1:], jnp.float32),
            pltpu.VMEM((rows + taps - 1, cols + 8, chans), jnp.float32),
        ],
        cost_estimate=pl.CostEstimate(
            flops=2 * count * rows * cols * chans * taps * taps,
            transcendentals=0,
            bytes_accessed=strips.size * 2 + count * rows * cols * chans * 4,
        ),
    )(strips, kernel.astype(jnp.float32))


def exchange(block, axis, dim, width):
    count = lax.axis_size(axis)
    forward = [(i, i + 1) for i in range(count - 1)]
    backward = [(target, source) for source, target in forward]
    low = lax.ppermute(
        lax.slice_in_dim(block, block.shape[dim] - width, None, axis=dim), axis, forward
    )
    high = lax.ppermute(lax.slice_in_dim(block, 0, width, axis=dim), axis, backward)
    return jnp.concatenate([low, block, high], axis=dim)


def section_conv(block, kernel):
    reach = (kernel.shape[0] - 1) // 2
    cols = block.shape[1]
    band = 8
    tall = exchange(block, "row", 0, reach)
    middle = depthwise(tall[None], kernel, band - reach, cols - 2 * band)
    full = exchange(tall, "col", 1, reach)
    ends = jnp.stack([full[:, : band + 2 * reach], full[:, cols - band :]], axis=0)
    edge = depthwise(ends, kernel, 0, band)
    return jnp.concatenate([edge[0], middle[0], edge[1]], axis=1)


def local_section(field, raw, sigma, w_in, w_out):
    kernel = masked_kernel(raw, sigma)
    conv_out = section_conv(field, kernel)
    mean = jnp.mean(conv_out, axis=-1, keepdims=True)
    var = jnp.mean((conv_out - mean) ** 2, axis=-1, keepdims=True)
    normed = ((conv_out - mean) * lax.rsqrt(var + 1e-06)).astype(jnp.bfloat16)
    hidden = jax.nn.gelu(jnp.dot(normed, w_in, preferred_element_type=jnp.float32)).astype(
        jnp.bfloat16
    )
    mixed = jnp.dot(hidden, w_out, preferred_element_type=jnp.float32)
    return (field.astype(jnp.float32) + mixed).astype(jnp.bfloat16)


def blur_down(padded):
    rows = padded.shape[0] - 2
    cols = padded.shape[1] - 2
    padded = padded.astype(jnp.float32)
    upper = padded[0:rows].reshape(rows // 2, 2, cols + 2, -1)
    lower = padded[2 : rows + 2].reshape(rows // 2, 2, cols + 2, -1)
    vert = (upper[:, 0] + 3.0 * upper[:, 1] + 3.0 * lower[:, 0] + lower[:, 1]) / 8.0
    left = vert[:, 0:cols].reshape(rows // 2, cols // 2, 2, -1)
    right = vert[:, 2 : cols + 2].reshape(rows // 2, cols // 2, 2, -1)
    return (
        (left[:, :, 0] + 3.0 * left[:, :, 1] + 3.0 * right[:, :, 0] + right[:, :, 1]) / 8.0
    ).astype(jnp.bfloat16)


def on_device(
    image,
    raw_first,
    sigma_first,
    in_first,
    out_first,
    widen,
    raw_second,
    sigma_second,
    in_second,
    out_second,
):
    first = local_section(image, raw_first, sigma_first, in_first, out_first)
    first_cycle = padded_2(first, (("row", 0), ("col", 1)), 1)
    first_pooled = blur_down(first_cycle)
    widened = jnp.dot(first_pooled, widen, preferred_element_type=jnp.float32).astype(jnp.bfloat16)
    second = local_section(widened, raw_second, sigma_second, in_second, out_second)
    second_cycle = padded_2(second, (("row", 0), ("col", 1)), 1)
    return blur_down(second_cycle)


def solution(mesh):
    placed = (P("row", "col", None), P(), P(), P(), P(), P(), P(), P(), P(), P())
    return jax.shard_map(
        on_device, mesh=mesh, in_specs=placed, out_specs=P("row", "col", None), check_vma=False
    )
```

```python
import functools

import jax
import jax.numpy as jnp
from jax import lax
from jax.experimental import pallas as pl
from jax.experimental.pallas import tpu as pltpu
from jax.sharding import PartitionSpec as P


def padded_2(block, sides, width):
    for axis, dim in sides:
        count = lax.axis_size(axis)
        forward = [(i, i + 1) for i in range(count - 1)]
        backward = [(target, source) for source, target in forward]
        low = lax.ppermute(
            lax.slice_in_dim(block, block.shape[dim] - width, None, axis=dim), axis, forward
        )
        high = lax.ppermute(lax.slice_in_dim(block, 0, width, axis=dim), axis, backward)
        block = jnp.concatenate([low, block, high], axis=dim)
    return block


def masked_kernel(raw, sigma):
    offsets = jnp.arange(raw.shape[0]).astype(jnp.float32) - 7.0
    dist = offsets[:, None] ** 2 + offsets[None, :] ** 2
    mask = jnp.exp(-dist[:, :, None] / (2.0 * sigma[None, None, :] ** 2))
    return (raw * mask).astype(jnp.bfloat16)


def _dw_body(x_all, k_ref, o_all, xf_ref, xs_ref, *, taps, cbase, rows, cols, chans, rb):
    nlb = chans // 128
    njb = cols // 8
    nrb = rows // rb
    spread = max(1, min(8, 16 // (njb * nlb)))

    def one_strip(n, carry):
        x_ref = x_all.at[n]
        o_ref = o_all.at[n]

        def widen_row(r, c):
            xf_ref[r] = x_ref[r].astype(jnp.float32)
            return c

        lax.fori_loop(0, rows + taps - 1, widen_row, 0, unroll=spread)
        first = True
        for s in range(8):
            if cbase + s == 0:
                src = xf_ref
            else:
                width = cols + 8 if s + 8 < taps else cols

                def shift(r, c, s=s, width=width):
                    xs_ref[r, pl.ds(0, width), :] = xf_ref[r, pl.ds(cbase + s, width), :]
                    return c

                lax.fori_loop(0, rows + taps - 1, shift, 0, unroll=spread)
                src = xs_ref
            for q in range(2):
                b = 8 * q + s
                if b >= taps:
                    continue
                for lb in range(nlb):
                    lanes = pl.ds(lb * 128, 128)
                    ks = [
                        jnp.broadcast_to(k_ref[a, pl.ds(b, 1), lanes], (8, 128))
                        for a in range(taps)
                    ]

                    def body(i, c, src=src, q=q, ks=ks, lanes=lanes, first=first):
                        r0 = pl.multiple_of((i // njb) * rb, rb)
                        j0 = pl.multiple_of((i % njb) * 8, 8)
                        xs = src[pl.ds(r0, rb + taps - 1), pl.ds(j0 + 8 * q, 8), lanes]
                        if first:
                            acc = jnp.zeros((rb, 8, 128), jnp.float32)
                        else:
                            acc = o_ref[pl.ds(r0, rb), pl.ds(j0, 8), lanes]
                        terms = [xs[a : a + rb] * ks[a][None] for a in range(taps)]
                        for g in range(0, taps, 5):
                            group = terms[g : g + 5]
                            while len(group) > 1:
                                group = [
                                    group[i] + group[i + 1] if i + 1 < len(group) else group[i]
                                    for i in range(0, len(group), 2)
                                ]
                            acc = acc + group[0]
                        o_ref[pl.ds(r0, rb), pl.ds(j0, 8), lanes] = acc
                        return c

                    lax.fori_loop(0, nrb * njb, body, 0, unroll=2)
                first = False
        return carry

    lax.fori_loop(0, x_all.shape[0], one_strip, 0)


def depthwise(strips, kernel, cbase, cols):
    taps = kernel.shape[0]
    count = strips.shape[0]
    rows = strips.shape[1] - taps + 1
    chans = strips.shape[3]
    body = functools.partial(
        _dw_body, taps=taps, cbase=cbase, rows=rows, cols=cols, chans=chans, rb=8
    )
    vmem = pl.BlockSpec(memory_space=pltpu.VMEM)
    return pl.pallas_call(
        body,
        out_shape=jax.ShapeDtypeStruct((count, rows, cols, chans), jnp.float32),
        in_specs=[vmem, vmem],
        out_specs=vmem,
        scratch_shapes=[
            pltpu.VMEM(strips.shape[1:], jnp.float32),
            pltpu.VMEM((rows + taps - 1, cols + 8, chans), jnp.float32),
        ],
        cost_estimate=pl.CostEstimate(
            flops=2 * count * rows * cols * chans * taps * taps,
            transcendentals=0,
            bytes_accessed=strips.size * 2 + count * rows * cols * chans * 4,
        ),
    )(strips, kernel.astype(jnp.float32))


def exchange(block, axis, dim, width):
    count = lax.axis_size(axis)
    forward = [(i, i + 1) for i in range(count - 1)]
    backward = [(target, source) for source, target in forward]
    low = lax.ppermute(
        lax.slice_in_dim(block, block.shape[dim] - width, None, axis=dim), axis, forward
    )
    high = lax.ppermute(lax.slice_in_dim(block, 0, width, axis=dim), axis, backward)
    return jnp.concatenate([low, block, high], axis=dim)


def section_conv(block, kernel):
    reach = (kernel.shape[0] - 1) // 2
    cols = block.shape[1]
    band = 8
    tall = exchange(block, "row", 0, reach)
    middle = depthwise(tall[None], kernel, band - reach, cols - 2 * band)
    full = exchange(tall, "col", 1, reach)
    ends = jnp.stack([full[:, : band + 2 * reach], full[:, cols - band :]], axis=0)
    edge = depthwise(ends, kernel, 0, band)
    return jnp.concatenate([edge[0], middle[0], edge[1]], axis=1)


def local_section(field, raw, sigma, w_in, w_out):
    kernel = masked_kernel(raw, sigma)
    conv_out = section_conv(field, kernel)
    mean = jnp.mean(conv_out, axis=-1, keepdims=True)
    var = jnp.mean((conv_out - mean) ** 2, axis=-1, keepdims=True)
    normed = ((conv_out - mean) * lax.rsqrt(var + 1e-06)).astype(jnp.bfloat16)
    hidden = jax.nn.gelu(jnp.dot(normed, w_in, preferred_element_type=jnp.float32)).astype(
        jnp.bfloat16
    )
    mixed = jnp.dot(hidden, w_out, preferred_element_type=jnp.float32)
    return (field.astype(jnp.float32) + mixed).astype(jnp.bfloat16)


def blur_down(padded):
    rows = padded.shape[0] - 2
    cols = padded.shape[1] - 2
    padded = padded.astype(jnp.float32)
    upper = padded[0:rows].reshape(rows // 2, 2, cols + 2, -1)
    lower = padded[2 : rows + 2].reshape(rows // 2, 2, cols + 2, -1)
    vert = (upper[:, 0] + 3.0 * upper[:, 1] + 3.0 * lower[:, 0] + lower[:, 1]) / 8.0
    left = vert[:, 0:cols].reshape(rows // 2, cols // 2, 2, -1)
    right = vert[:, 2 : cols + 2].reshape(rows // 2, cols // 2, 2, -1)
    return (
        (left[:, :, 0] + 3.0 * left[:, :, 1] + 3.0 * right[:, :, 0] + right[:, :, 1]) / 8.0
    ).astype(jnp.bfloat16)


def on_device(
    image,
    raw_first,
    sigma_first,
    in_first,
    out_first,
    widen,
    raw_second,
    sigma_second,
    in_second,
    out_second,
):
    first = local_section(image, raw_first, sigma_first, in_first, out_first)
    first_cycle = padded_2(first, (("row", 0), ("col", 1)), 1)
    first_pooled = blur_down(first_cycle)
    widened = jnp.dot(first_pooled, widen, preferred_element_type=jnp.float32).astype(jnp.bfloat16)
    second = local_section(widened, raw_second, sigma_second, in_second, out_second)
    second_cycle = padded_2(second, (("row", 0), ("col", 1)), 1)
    return blur_down(second_cycle)


def solution(mesh):
    placed = (P("row", "col", None), P(), P(), P(), P(), P(), P(), P(), P(), P())
    return jax.shard_map(
        on_device, mesh=mesh, in_specs=placed, out_specs=P("row", "col", None), check_vma=False
    )
```

```python
import functools

import jax
import jax.numpy as jnp
from jax import lax
from jax.experimental import pallas as pl
from jax.experimental.pallas import tpu as pltpu
from jax.sharding import PartitionSpec as P


def padded_2(block, sides, width):
    for axis, dim in sides:
        count = lax.axis_size(axis)
        forward = [(i, i + 1) for i in range(count - 1)]
        backward = [(target, source) for source, target in forward]
        low = lax.ppermute(
            lax.slice_in_dim(block, block.shape[dim] - width, None, axis=dim), axis, forward
        )
        high = lax.ppermute(lax.slice_in_dim(block, 0, width, axis=dim), axis, backward)
        block = jnp.concatenate([low, block, high], axis=dim)
    return block


def masked_kernel(raw, sigma):
    offsets = jnp.arange(raw.shape[0]).astype(jnp.float32) - 7.0
    dist = offsets[:, None] ** 2 + offsets[None, :] ** 2
    mask = jnp.exp(-dist[:, :, None] / (2.0 * sigma[None, None, :] ** 2))
    return (raw * mask).astype(jnp.bfloat16)


def _dw_body(x_all, k_ref, o_all, xf_ref, xs_ref, *, taps, cbase, rows, cols, chans, rb):
    nlb = chans // 128
    njb = cols // 8
    nrb = rows // rb
    spread = max(1, min(8, 16 // (njb * nlb)))

    def one_strip(n, carry):
        x_ref = x_all.at[n]
        o_ref = o_all.at[n]

        def widen_row(r, c):
            xf_ref[r] = x_ref[r].astype(jnp.float32)
            return c

        lax.fori_loop(0, rows + taps - 1, widen_row, 0, unroll=spread)
        first = True
        for s in range(8):
            if (cbase + s) % 8 == 0:
                src, off = xf_ref, cbase + s
            else:
                off = 0
                width = cols + 8 if s + 8 < taps else cols

                def shift(r, c, s=s, width=width):
                    xs_ref[r, pl.ds(0, width), :] = xf_ref[r, pl.ds(cbase + s, width), :]
                    return c

                lax.fori_loop(0, rows + taps - 1, shift, 0, unroll=spread)
                src = xs_ref
            for q in range(2):
                b = 8 * q + s
                if b >= taps:
                    continue
                for lb in range(nlb):
                    lanes = pl.ds(lb * 128, 128)
                    ks = [
                        jnp.broadcast_to(k_ref[a, pl.ds(b, 1), lanes], (8, 128))
                        for a in range(taps)
                    ]

                    def body(i, c, src=src, off=off, q=q, ks=ks, lanes=lanes, first=first):
                        r0 = pl.multiple_of((i // njb) * rb, rb)
                        j0 = pl.multiple_of((i % njb) * 8, 8)
                        xs = src[pl.ds(r0, rb + taps - 1), pl.ds(j0 + off + 8 * q, 8), lanes]
                        if first:
                            acc = jnp.zeros((rb, 8, 128), jnp.float32)
                        else:
                            acc = o_ref[pl.ds(r0, rb), pl.ds(j0, 8), lanes]
                        terms = [xs[a : a + rb] * ks[a][None] for a in range(taps)]
                        for g in range(0, taps, 5):
                            group = terms[g : g + 5]
                            while len(group) > 1:
                                group = [
                                    group[i] + group[i + 1] if i + 1 < len(group) else group[i]
                                    for i in range(0, len(group), 2)
                                ]
                            acc = acc + group[0]
                        o_ref[pl.ds(r0, rb), pl.ds(j0, 8), lanes] = acc
                        return c

                    lax.fori_loop(0, nrb * njb, body, 0, unroll=2)
                first = False
        return carry

    lax.fori_loop(0, x_all.shape[0], one_strip, 0)


def depthwise(strips, kernel, cbase, cols):
    taps = kernel.shape[0]
    count = strips.shape[0]
    rows = strips.shape[1] - taps + 1
    chans = strips.shape[3]
    body = functools.partial(
        _dw_body, taps=taps, cbase=cbase, rows=rows, cols=cols, chans=chans, rb=8
    )
    vmem = pl.BlockSpec(memory_space=pltpu.VMEM)
    return pl.pallas_call(
        body,
        out_shape=jax.ShapeDtypeStruct((count, rows, cols, chans), jnp.float32),
        in_specs=[vmem, vmem],
        out_specs=vmem,
        scratch_shapes=[
            pltpu.VMEM(strips.shape[1:], jnp.float32),
            pltpu.VMEM((rows + taps - 1, cols + 8, chans), jnp.float32),
        ],
        cost_estimate=pl.CostEstimate(
            flops=2 * count * rows * cols * chans * taps * taps,
            transcendentals=0,
            bytes_accessed=strips.size * 2 + count * rows * cols * chans * 4,
        ),
    )(strips, kernel.astype(jnp.float32))


def exchange(block, axis, dim, width):
    count = lax.axis_size(axis)
    forward = [(i, i + 1) for i in range(count - 1)]
    backward = [(target, source) for source, target in forward]
    low = lax.ppermute(
        lax.slice_in_dim(block, block.shape[dim] - width, None, axis=dim), axis, forward
    )
    high = lax.ppermute(lax.slice_in_dim(block, 0, width, axis=dim), axis, backward)
    return jnp.concatenate([low, block, high], axis=dim)


def section_conv(block, kernel):
    reach = (kernel.shape[0] - 1) // 2
    cols = block.shape[1]
    band = 8
    tall = exchange(block, "row", 0, reach)
    middle = depthwise(tall[None], kernel, band - reach, cols - 2 * band)
    full = exchange(tall, "col", 1, reach)
    ends = jnp.stack([full[:, : band + 2 * reach], full[:, cols - band :]], axis=0)
    edge = depthwise(ends, kernel, 0, band)
    return jnp.concatenate([edge[0], middle[0], edge[1]], axis=1)


def local_section(field, raw, sigma, w_in, w_out):
    kernel = masked_kernel(raw, sigma)
    conv_out = section_conv(field, kernel)
    mean = jnp.mean(conv_out, axis=-1, keepdims=True)
    var = jnp.mean((conv_out - mean) ** 2, axis=-1, keepdims=True)
    normed = ((conv_out - mean) * lax.rsqrt(var + 1e-06)).astype(jnp.bfloat16)
    hidden = jax.nn.gelu(jnp.dot(normed, w_in, preferred_element_type=jnp.float32)).astype(
        jnp.bfloat16
    )
    mixed = jnp.dot(hidden, w_out, preferred_element_type=jnp.float32)
    return (field.astype(jnp.float32) + mixed).astype(jnp.bfloat16)


def blur_down(padded):
    rows = padded.shape[0] - 2
    cols = padded.shape[1] - 2
    padded = padded.astype(jnp.float32)
    upper = padded[0:rows].reshape(rows // 2, 2, cols + 2, -1)
    lower = padded[2 : rows + 2].reshape(rows // 2, 2, cols + 2, -1)
    vert = (upper[:, 0] + 3.0 * upper[:, 1] + 3.0 * lower[:, 0] + lower[:, 1]) / 8.0
    left = vert[:, 0:cols].reshape(rows // 2, cols // 2, 2, -1)
    right = vert[:, 2 : cols + 2].reshape(rows // 2, cols // 2, 2, -1)
    return (
        (left[:, :, 0] + 3.0 * left[:, :, 1] + 3.0 * right[:, :, 0] + right[:, :, 1]) / 8.0
    ).astype(jnp.bfloat16)


def on_device(
    image,
    raw_first,
    sigma_first,
    in_first,
    out_first,
    widen,
    raw_second,
    sigma_second,
    in_second,
    out_second,
):
    first = local_section(image, raw_first, sigma_first, in_first, out_first)
    first_cycle = padded_2(first, (("row", 0), ("col", 1)), 1)
    first_pooled = blur_down(first_cycle)
    widened = jnp.dot(first_pooled, widen, preferred_element_type=jnp.float32).astype(jnp.bfloat16)
    second = local_section(widened, raw_second, sigma_second, in_second, out_second)
    second_cycle = padded_2(second, (("row", 0), ("col", 1)), 1)
    return blur_down(second_cycle)


def solution(mesh):
    placed = (P("row", "col", None), P(), P(), P(), P(), P(), P(), P(), P(), P())
    return jax.shard_map(
        on_device, mesh=mesh, in_specs=placed, out_specs=P("row", "col", None), check_vma=False
    )
```

```python
import functools

import jax
import jax.numpy as jnp
from jax import lax
from jax.experimental import pallas as pl
from jax.experimental.pallas import tpu as pltpu
from jax.sharding import PartitionSpec as P


def padded_2(block, sides, width):
    for axis, dim in sides:
        count = lax.axis_size(axis)
        forward = [(i, i + 1) for i in range(count - 1)]
        backward = [(target, source) for source, target in forward]
        low = lax.ppermute(
            lax.slice_in_dim(block, block.shape[dim] - width, None, axis=dim), axis, forward
        )
        high = lax.ppermute(lax.slice_in_dim(block, 0, width, axis=dim), axis, backward)
        block = jnp.concatenate([low, block, high], axis=dim)
    return block


def masked_kernel(raw, sigma):
    offsets = jnp.arange(raw.shape[0]).astype(jnp.float32) - 7.0
    dist = offsets[:, None] ** 2 + offsets[None, :] ** 2
    mask = jnp.exp(-dist[:, :, None] / (2.0 * sigma[None, None, :] ** 2))
    return (raw * mask).astype(jnp.bfloat16)


def _dw_body(x_all, k_ref, o_all, xf_ref, xs_ref, *, taps, cbase, rows, cols, chans, rb):
    nlb = chans // 128
    njb = cols // 8
    nrb = rows // rb
    spread = max(1, min(8, 16 // (njb * nlb)))

    def one_strip(n, carry):
        x_ref = x_all.at[n]
        o_ref = o_all.at[n]

        def widen_row(r, c):
            xf_ref[r] = x_ref[r].astype(jnp.float32)
            return c

        lax.fori_loop(0, rows + taps - 1, widen_row, 0, unroll=spread)
        first = True
        for s in range(8):
            if (cbase + s) % 8 == 0:
                src, off = xf_ref, cbase + s
            else:
                off = 0
                width = cols + 8 if s + 8 < taps else cols

                def shift(r, c, s=s, width=width):
                    xs_ref[r, pl.ds(0, width), :] = xf_ref[r, pl.ds(cbase + s, width), :]
                    return c

                lax.fori_loop(0, rows + taps - 1, shift, 0, unroll=spread)
                src = xs_ref
            for q in range(2):
                b = 8 * q + s
                if b >= taps:
                    continue
                for lb in range(nlb):
                    lanes = pl.ds(lb * 128, 128)
                    ks = [
                        jnp.broadcast_to(k_ref[a, pl.ds(b, 1), lanes], (8, 128))
                        for a in range(taps)
                    ]

                    def body(i, c, src=src, off=off, q=q, ks=ks, lanes=lanes, first=first):
                        r0 = pl.multiple_of((i // njb) * rb, rb)
                        j0 = pl.multiple_of((i % njb) * 8, 8)
                        xs = src[pl.ds(r0, rb + taps - 1), pl.ds(j0 + off + 8 * q, 8), lanes]
                        if first:
                            acc = jnp.zeros((rb, 8, 128), jnp.float32)
                        else:
                            acc = o_ref[pl.ds(r0, rb), pl.ds(j0, 8), lanes]
                        terms = [xs[a : a + rb] * ks[a][None] for a in range(taps)]
                        for g in range(0, taps, 5):
                            group = terms[g : g + 5]
                            while len(group) > 1:
                                group = [
                                    group[i] + group[i + 1] if i + 1 < len(group) else group[i]
                                    for i in range(0, len(group), 2)
                                ]
                            acc = acc + group[0]
                        o_ref[pl.ds(r0, rb), pl.ds(j0, 8), lanes] = acc
                        return c

                    lax.fori_loop(0, nrb * njb, body, 0, unroll=2)
                first = False
        return carry

    lax.fori_loop(0, x_all.shape[0], one_strip, 0)


def depthwise(strips, kernel, cbase, cols):
    taps = kernel.shape[0]
    count = strips.shape[0]
    rows = strips.shape[1] - taps + 1
    chans = strips.shape[3]
    body = functools.partial(
        _dw_body, taps=taps, cbase=cbase, rows=rows, cols=cols, chans=chans, rb=8
    )
    vmem = pl.BlockSpec(memory_space=pltpu.VMEM)
    return pl.pallas_call(
        body,
        out_shape=jax.ShapeDtypeStruct((count, rows, cols, chans), jnp.float32),
        in_specs=[vmem, vmem],
        out_specs=vmem,
        scratch_shapes=[
            pltpu.VMEM(strips.shape[1:], jnp.float32),
            pltpu.VMEM((rows + taps - 1, cols + 8, chans), jnp.float32),
        ],
        cost_estimate=pl.CostEstimate(
            flops=2 * count * rows * cols * chans * taps * taps,
            transcendentals=0,
            bytes_accessed=strips.size * 2 + count * rows * cols * chans * 4,
        ),
    )(strips, kernel.astype(jnp.float32))


def exchange(block, axis, dim, width):
    count = lax.axis_size(axis)
    forward = [(i, i + 1) for i in range(count - 1)]
    backward = [(target, source) for source, target in forward]
    low = lax.ppermute(
        lax.slice_in_dim(block, block.shape[dim] - width, None, axis=dim), axis, forward
    )
    high = lax.ppermute(lax.slice_in_dim(block, 0, width, axis=dim), axis, backward)
    return jnp.concatenate([low, block, high], axis=dim)


def section_conv(block, kernel, split_rows):
    reach = (kernel.shape[0] - 1) // 2
    rows, cols = block.shape[:2]
    band = 8
    tall = exchange(block, "row", 0, reach)
    if split_rows:
        inner = depthwise(block[band - reach : rows - band + reach][None], kernel, 1, cols - 2 * band)
        caps = jnp.stack([tall[: band + 2 * reach], tall[rows - band :]], axis=0)
        caps = depthwise(caps, kernel, band - reach, cols - 2 * band)
        middle = jnp.concatenate([caps[0], inner[0], caps[1]], axis=0)
    else:
        middle = depthwise(tall[None], kernel, band - reach, cols - 2 * band)[0]
    full = exchange(tall, "col", 1, reach)
    ends = jnp.stack([full[:, : band + 2 * reach], full[:, cols - band :]], axis=0)
    edge = depthwise(ends, kernel, 0, band)
    return jnp.concatenate([edge[0], middle, edge[1]], axis=1)


def local_section(field, raw, sigma, w_in, w_out, split_rows):
    kernel = masked_kernel(raw, sigma)
    conv_out = section_conv(field, kernel, split_rows)
    mean = jnp.mean(conv_out, axis=-1, keepdims=True)
    var = jnp.mean((conv_out - mean) ** 2, axis=-1, keepdims=True)
    normed = ((conv_out - mean) * lax.rsqrt(var + 1e-06)).astype(jnp.bfloat16)
    hidden = jax.nn.gelu(jnp.dot(normed, w_in, preferred_element_type=jnp.float32)).astype(
        jnp.bfloat16
    )
    mixed = jnp.dot(hidden, w_out, preferred_element_type=jnp.float32)
    return (field.astype(jnp.float32) + mixed).astype(jnp.bfloat16)


def blur_down(padded):
    rows = padded.shape[0] - 2
    cols = padded.shape[1] - 2
    padded = padded.astype(jnp.float32)
    upper = padded[0:rows].reshape(rows // 2, 2, cols + 2, -1)
    lower = padded[2 : rows + 2].reshape(rows // 2, 2, cols + 2, -1)
    vert = (upper[:, 0] + 3.0 * upper[:, 1] + 3.0 * lower[:, 0] + lower[:, 1]) / 8.0
    left = vert[:, 0:cols].reshape(rows // 2, cols // 2, 2, -1)
    right = vert[:, 2 : cols + 2].reshape(rows // 2, cols // 2, 2, -1)
    return (
        (left[:, :, 0] + 3.0 * left[:, :, 1] + 3.0 * right[:, :, 0] + right[:, :, 1]) / 8.0
    ).astype(jnp.bfloat16)


def on_device(
    image,
    raw_first,
    sigma_first,
    in_first,
    out_first,
    widen,
    raw_second,
    sigma_second,
    in_second,
    out_second,
):
    first = local_section(image, raw_first, sigma_first, in_first, out_first, True)
    first_cycle = padded_2(first, (("row", 0), ("col", 1)), 1)
    first_pooled = blur_down(first_cycle)
    widened = jnp.dot(first_pooled, widen, preferred_element_type=jnp.float32).astype(jnp.bfloat16)
    second = local_section(widened, raw_second, sigma_second, in_second, out_second, False)
    second_cycle = padded_2(second, (("row", 0), ("col", 1)), 1)
    return blur_down(second_cycle)


def solution(mesh):
    placed = (P("row", "col", None), P(), P(), P(), P(), P(), P(), P(), P(), P())
    return jax.shard_map(
        on_device, mesh=mesh, in_specs=placed, out_specs=P("row", "col", None), check_vma=False
    )
```

```python
import functools

import jax
import jax.numpy as jnp
from jax import lax
from jax.experimental import pallas as pl
from jax.experimental.pallas import tpu as pltpu
from jax.sharding import PartitionSpec as P


def padded_2(block, sides, width):
    for axis, dim in sides:
        count = lax.axis_size(axis)
        forward = [(i, i + 1) for i in range(count - 1)]
        backward = [(target, source) for source, target in forward]
        low = lax.ppermute(
            lax.slice_in_dim(block, block.shape[dim] - width, None, axis=dim), axis, forward
        )
        high = lax.ppermute(lax.slice_in_dim(block, 0, width, axis=dim), axis, backward)
        block = jnp.concatenate([low, block, high], axis=dim)
    return block


def masked_kernel(raw, sigma):
    offsets = jnp.arange(raw.shape[0]).astype(jnp.float32) - 7.0
    dist = offsets[:, None] ** 2 + offsets[None, :] ** 2
    mask = jnp.exp(-dist[:, :, None] / (2.0 * sigma[None, None, :] ** 2))
    return (raw * mask).astype(jnp.bfloat16)


def _dw_body(*refs, parts, taps, cbase, rows, cols, chans, rb):
    x_parts = refs[:parts]
    k_ref, o_all, xf_ref, xs_ref = refs[parts:]
    nlb = chans // 128
    njb = cols // 8
    nrb = rows // rb
    spread = max(1, min(8, 16 // (njb * nlb)))

    def one_strip(n, carry):
        o_ref = o_all.at[n]
        start = 0
        for x_all in x_parts:

            def widen_row(r, c, x_ref=x_all.at[n], start=start):
                xf_ref[start + r] = x_ref[r].astype(jnp.float32)
                return c

            lax.fori_loop(0, x_all.shape[1], widen_row, 0, unroll=spread)
            start += x_all.shape[1]
        first = True
        for s in range(8):
            if (cbase + s) % 8 == 0:
                src, off = xf_ref, cbase + s
            else:
                off = 0
                width = cols + 8 if s + 8 < taps else cols

                def shift(r, c, s=s, width=width):
                    xs_ref[r, pl.ds(0, width), :] = xf_ref[r, pl.ds(cbase + s, width), :]
                    return c

                lax.fori_loop(0, rows + taps - 1, shift, 0, unroll=spread)
                src = xs_ref
            for q in range(2):
                b = 8 * q + s
                if b >= taps:
                    continue
                for lb in range(nlb):
                    lanes = pl.ds(lb * 128, 128)
                    ks = [
                        jnp.broadcast_to(k_ref[a, pl.ds(b, 1), lanes], (8, 128))
                        for a in range(taps)
                    ]

                    def body(i, c, src=src, off=off, q=q, ks=ks, lanes=lanes, first=first):
                        r0 = pl.multiple_of((i // njb) * rb, rb)
                        j0 = pl.multiple_of((i % njb) * 8, 8)
                        xs = src[pl.ds(r0, rb + taps - 1), pl.ds(j0 + off + 8 * q, 8), lanes]
                        if first:
                            acc = jnp.zeros((rb, 8, 128), jnp.float32)
                        else:
                            acc = o_ref[pl.ds(r0, rb), pl.ds(j0, 8), lanes]
                        terms = [xs[a : a + rb] * ks[a][None] for a in range(taps)]
                        for g in range(0, taps, 5):
                            group = terms[g : g + 5]
                            while len(group) > 1:
                                group = [
                                    group[i] + group[i + 1] if i + 1 < len(group) else group[i]
                                    for i in range(0, len(group), 2)
                                ]
                            acc = acc + group[0]
                        o_ref[pl.ds(r0, rb), pl.ds(j0, 8), lanes] = acc
                        return c

                    lax.fori_loop(0, nrb * njb, body, 0, unroll=2)
                first = False
        return carry

    lax.fori_loop(0, x_parts[0].shape[0], one_strip, 0)


def depthwise(parts, kernel, cbase, cols):
    taps = kernel.shape[0]
    count = parts[0].shape[0]
    in_rows = sum(p.shape[1] for p in parts)
    rows = in_rows - taps + 1
    chans = parts[0].shape[3]
    body = functools.partial(
        _dw_body,
        parts=len(parts),
        taps=taps,
        cbase=cbase,
        rows=rows,
        cols=cols,
        chans=chans,
        rb=8,
    )
    vmem = pl.BlockSpec(memory_space=pltpu.VMEM)
    return pl.pallas_call(
        body,
        out_shape=jax.ShapeDtypeStruct((count, rows, cols, chans), jnp.float32),
        in_specs=[vmem] * (len(parts) + 1),
        out_specs=vmem,
        scratch_shapes=[
            pltpu.VMEM((in_rows,) + parts[0].shape[2:], jnp.float32),
            pltpu.VMEM((in_rows, cols + 8, chans), jnp.float32),
        ],
        cost_estimate=pl.CostEstimate(
            flops=2 * count * rows * cols * chans * taps * taps,
            transcendentals=0,
            bytes_accessed=sum(p.size for p in parts) * 2 + count * rows * cols * chans * 4,
        ),
    )(*parts, kernel.astype(jnp.float32))


def halos(block, axis, dim, width):
    count = lax.axis_size(axis)
    forward = [(i, i + 1) for i in range(count - 1)]
    backward = [(target, source) for source, target in forward]
    low = lax.ppermute(
        lax.slice_in_dim(block, block.shape[dim] - width, None, axis=dim), axis, forward
    )
    high = lax.ppermute(lax.slice_in_dim(block, 0, width, axis=dim), axis, backward)
    return low, high


def section_conv(block, kernel):
    reach = (kernel.shape[0] - 1) // 2
    cols = block.shape[1]
    band = 8
    up, down = halos(block, "row", 0, reach)
    pieces = [up, block, down]
    middle = depthwise([p[None] for p in pieces], kernel, band - reach, cols - 2 * band)

    def tall_cols(start, stop):
        return jnp.concatenate([p[:, start:stop] for p in pieces], axis=0)

    count = lax.axis_size("col")
    forward = [(i, i + 1) for i in range(count - 1)]
    backward = [(target, source) for source, target in forward]
    left = lax.ppermute(tall_cols(cols - reach, cols), "col", forward)
    right = lax.ppermute(tall_cols(0, reach), "col", backward)
    ends = jnp.stack(
        [
            jnp.concatenate([left, tall_cols(0, band + reach)], axis=1),
            jnp.concatenate([tall_cols(cols - band - reach, cols), right], axis=1),
        ],
        axis=0,
    )
    edge = depthwise([ends], kernel, 0, band)
    return jnp.concatenate([edge[0], middle[0], edge[1]], axis=1)


def local_section(field, raw, sigma, w_in, w_out):
    kernel = masked_kernel(raw, sigma)
    conv_out = section_conv(field, kernel)
    mean = jnp.mean(conv_out, axis=-1, keepdims=True)
    var = jnp.mean((conv_out - mean) ** 2, axis=-1, keepdims=True)
    normed = ((conv_out - mean) * lax.rsqrt(var + 1e-06)).astype(jnp.bfloat16)
    hidden = jax.nn.gelu(jnp.dot(normed, w_in, preferred_element_type=jnp.float32)).astype(
        jnp.bfloat16
    )
    mixed = jnp.dot(hidden, w_out, preferred_element_type=jnp.float32)
    return (field.astype(jnp.float32) + mixed).astype(jnp.bfloat16)


def blur_down(padded):
    rows = padded.shape[0] - 2
    cols = padded.shape[1] - 2
    padded = padded.astype(jnp.float32)
    upper = padded[0:rows].reshape(rows // 2, 2, cols + 2, -1)
    lower = padded[2 : rows + 2].reshape(rows // 2, 2, cols + 2, -1)
    vert = (upper[:, 0] + 3.0 * upper[:, 1] + 3.0 * lower[:, 0] + lower[:, 1]) / 8.0
    left = vert[:, 0:cols].reshape(rows // 2, cols // 2, 2, -1)
    right = vert[:, 2 : cols + 2].reshape(rows // 2, cols // 2, 2, -1)
    return (
        (left[:, :, 0] + 3.0 * left[:, :, 1] + 3.0 * right[:, :, 0] + right[:, :, 1]) / 8.0
    ).astype(jnp.bfloat16)


def on_device(
    image,
    raw_first,
    sigma_first,
    in_first,
    out_first,
    widen,
    raw_second,
    sigma_second,
    in_second,
    out_second,
):
    first = local_section(image, raw_first, sigma_first, in_first, out_first)
    first_cycle = padded_2(first, (("row", 0), ("col", 1)), 1)
    first_pooled = blur_down(first_cycle)
    widened = jnp.dot(first_pooled, widen, preferred_element_type=jnp.float32).astype(jnp.bfloat16)
    second = local_section(widened, raw_second, sigma_second, in_second, out_second)
    second_cycle = padded_2(second, (("row", 0), ("col", 1)), 1)
    return blur_down(second_cycle)


def solution(mesh):
    placed = (P("row", "col", None), P(), P(), P(), P(), P(), P(), P(), P(), P())
    return jax.shard_map(
        on_device, mesh=mesh, in_specs=placed, out_specs=P("row", "col", None), check_vma=False
    )
```

```python
import functools

import jax
import jax.numpy as jnp
from jax import lax
from jax.experimental import pallas as pl
from jax.experimental.pallas import tpu as pltpu
from jax.sharding import PartitionSpec as P


def padded_2(block, sides, width):
    for axis, dim in sides:
        count = lax.axis_size(axis)
        forward = [(i, i + 1) for i in range(count - 1)]
        backward = [(target, source) for source, target in forward]
        low = lax.ppermute(
            lax.slice_in_dim(block, block.shape[dim] - width, None, axis=dim), axis, forward
        )
        high = lax.ppermute(lax.slice_in_dim(block, 0, width, axis=dim), axis, backward)
        block = jnp.concatenate([low, block, high], axis=dim)
    return block


def masked_kernel(raw, sigma):
    offsets = jnp.arange(raw.shape[0]).astype(jnp.float32) - 7.0
    dist = offsets[:, None] ** 2 + offsets[None, :] ** 2
    mask = jnp.exp(-dist[:, :, None] / (2.0 * sigma[None, None, :] ** 2))
    return (raw * mask).astype(jnp.bfloat16)


def _dw_body(*refs, parts, taps, cbase, rows, cols, chans, rb):
    x_parts = refs[:parts]
    k_ref, o_all, xf_ref, xs_ref = refs[parts:]
    nlb = chans // 128
    njb = cols // 8
    nrb = rows // rb
    spread = max(1, min(8, 32 // (njb * nlb)))

    def one_strip(n, carry):
        o_ref = o_all.at[n]
        start = 0
        for x_all in x_parts:

            def widen_row(r, c, x_ref=x_all.at[n], start=start):
                xf_ref[start + r] = x_ref[r].astype(jnp.float32)
                return c

            lax.fori_loop(0, x_all.shape[1], widen_row, 0, unroll=spread)
            start += x_all.shape[1]
        first = True
        for s in range(8):
            if (cbase + s) % 8 == 0:
                src, off = xf_ref, cbase + s
            else:
                off = 0
                width = cols + 8 if s + 8 < taps else cols

                def shift(r, c, s=s, width=width):
                    xs_ref[r, pl.ds(0, width), :] = xf_ref[r, pl.ds(cbase + s, width), :]
                    return c

                lax.fori_loop(0, rows + taps - 1, shift, 0, unroll=spread)
                src = xs_ref
            for q in range(2):
                b = 8 * q + s
                if b >= taps:
                    continue
                for lb in range(nlb):
                    lanes = pl.ds(lb * 128, 128)
                    ks = [
                        jnp.broadcast_to(k_ref[a, pl.ds(b, 1), lanes], (8, 128))
                        for a in range(taps)
                    ]

                    def body(i, c, src=src, off=off, q=q, ks=ks, lanes=lanes, first=first):
                        r0 = pl.multiple_of((i // njb) * rb, rb)
                        j0 = pl.multiple_of((i % njb) * 8, 8)
                        xs = src[pl.ds(r0, rb + taps - 1), pl.ds(j0 + off + 8 * q, 8), lanes]
                        if first:
                            acc = jnp.zeros((rb, 8, 128), jnp.float32)
                        else:
                            acc = o_ref[pl.ds(r0, rb), pl.ds(j0, 8), lanes]
                        terms = [xs[a : a + rb] * ks[a][None] for a in range(taps)]
                        for g in range(0, taps, 5):
                            group = terms[g : g + 5]
                            while len(group) > 1:
                                group = [
                                    group[i] + group[i + 1] if i + 1 < len(group) else group[i]
                                    for i in range(0, len(group), 2)
                                ]
                            acc = acc + group[0]
                        o_ref[pl.ds(r0, rb), pl.ds(j0, 8), lanes] = acc
                        return c

                    lax.fori_loop(0, nrb * njb, body, 0, unroll=2)
                first = False
        return carry

    lax.fori_loop(0, x_parts[0].shape[0], one_strip, 0)


def depthwise(parts, kernel, cbase, cols):
    taps = kernel.shape[0]
    count = parts[0].shape[0]
    in_rows = sum(p.shape[1] for p in parts)
    rows = in_rows - taps + 1
    chans = parts[0].shape[3]
    body = functools.partial(
        _dw_body,
        parts=len(parts),
        taps=taps,
        cbase=cbase,
        rows=rows,
        cols=cols,
        chans=chans,
        rb=8,
    )
    vmem = pl.BlockSpec(memory_space=pltpu.VMEM)
    return pl.pallas_call(
        body,
        out_shape=jax.ShapeDtypeStruct((count, rows, cols, chans), jnp.float32),
        in_specs=[vmem] * (len(parts) + 1),
        out_specs=vmem,
        scratch_shapes=[
            pltpu.VMEM((in_rows,) + parts[0].shape[2:], jnp.float32),
            pltpu.VMEM((in_rows, cols + 8, chans), jnp.float32),
        ],
        cost_estimate=pl.CostEstimate(
            flops=2 * count * rows * cols * chans * taps * taps,
            transcendentals=0,
            bytes_accessed=sum(p.size for p in parts) * 2 + count * rows * cols * chans * 4,
        ),
    )(*parts, kernel.astype(jnp.float32))


def halos(block, axis, dim, width):
    count = lax.axis_size(axis)
    forward = [(i, i + 1) for i in range(count - 1)]
    backward = [(target, source) for source, target in forward]
    low = lax.ppermute(
        lax.slice_in_dim(block, block.shape[dim] - width, None, axis=dim), axis, forward
    )
    high = lax.ppermute(lax.slice_in_dim(block, 0, width, axis=dim), axis, backward)
    return low, high


def section_conv(block, kernel):
    reach = (kernel.shape[0] - 1) // 2
    cols = block.shape[1]
    band = 8
    up, down = halos(block, "row", 0, reach)
    pieces = [up, block, down]
    middle = depthwise([p[None] for p in pieces], kernel, band - reach, cols - 2 * band)

    def tall_cols(start, stop):
        return jnp.concatenate([p[:, start:stop] for p in pieces], axis=0)

    count = lax.axis_size("col")
    forward = [(i, i + 1) for i in range(count - 1)]
    backward = [(target, source) for source, target in forward]
    left = lax.ppermute(tall_cols(cols - reach, cols), "col", forward)
    right = lax.ppermute(tall_cols(0, reach), "col", backward)
    ends = jnp.stack(
        [
            jnp.concatenate([left, tall_cols(0, band + reach)], axis=1),
            jnp.concatenate([tall_cols(cols - band - reach, cols), right], axis=1),
        ],
        axis=0,
    )
    edge = depthwise([ends], kernel, 0, band)
    return jnp.concatenate([edge[0], middle[0], edge[1]], axis=1)


def local_section(field, raw, sigma, w_in, w_out):
    kernel = masked_kernel(raw, sigma)
    conv_out = section_conv(field, kernel)
    mean = jnp.mean(conv_out, axis=-1, keepdims=True)
    var = jnp.mean((conv_out - mean) ** 2, axis=-1, keepdims=True)
    normed = ((conv_out - mean) * lax.rsqrt(var + 1e-06)).astype(jnp.bfloat16)
    hidden = jax.nn.gelu(jnp.dot(normed, w_in, preferred_element_type=jnp.float32)).astype(
        jnp.bfloat16
    )
    mixed = jnp.dot(hidden, w_out, preferred_element_type=jnp.float32)
    return (field.astype(jnp.float32) + mixed).astype(jnp.bfloat16)


def blur_down(padded):
    rows = padded.shape[0] - 2
    cols = padded.shape[1] - 2
    padded = padded.astype(jnp.float32)
    upper = padded[0:rows].reshape(rows // 2, 2, cols + 2, -1)
    lower = padded[2 : rows + 2].reshape(rows // 2, 2, cols + 2, -1)
    vert = (upper[:, 0] + 3.0 * upper[:, 1] + 3.0 * lower[:, 0] + lower[:, 1]) / 8.0
    left = vert[:, 0:cols].reshape(rows // 2, cols // 2, 2, -1)
    right = vert[:, 2 : cols + 2].reshape(rows // 2, cols // 2, 2, -1)
    return (
        (left[:, :, 0] + 3.0 * left[:, :, 1] + 3.0 * right[:, :, 0] + right[:, :, 1]) / 8.0
    ).astype(jnp.bfloat16)


def on_device(
    image,
    raw_first,
    sigma_first,
    in_first,
    out_first,
    widen,
    raw_second,
    sigma_second,
    in_second,
    out_second,
):
    first = local_section(image, raw_first, sigma_first, in_first, out_first)
    first_cycle = padded_2(first, (("row", 0), ("col", 1)), 1)
    first_pooled = blur_down(first_cycle)
    widened = jnp.dot(first_pooled, widen, preferred_element_type=jnp.float32).astype(jnp.bfloat16)
    second = local_section(widened, raw_second, sigma_second, in_second, out_second)
    second_cycle = padded_2(second, (("row", 0), ("col", 1)), 1)
    return blur_down(second_cycle)


def solution(mesh):
    placed = (P("row", "col", None), P(), P(), P(), P(), P(), P(), P(), P(), P())
    return jax.shard_map(
        on_device, mesh=mesh, in_specs=placed, out_specs=P("row", "col", None), check_vma=False
    )
```

```python
import functools

import jax
import jax.numpy as jnp
from jax import lax
from jax.experimental import pallas as pl
from jax.experimental.pallas import tpu as pltpu
from jax.sharding import PartitionSpec as P


def padded_2(block, sides, width):
    for axis, dim in sides:
        count = lax.axis_size(axis)
        forward = [(i, i + 1) for i in range(count - 1)]
        backward = [(target, source) for source, target in forward]
        low = lax.ppermute(
            lax.slice_in_dim(block, block.shape[dim] - width, None, axis=dim), axis, forward
        )
        high = lax.ppermute(lax.slice_in_dim(block, 0, width, axis=dim), axis, backward)
        block = jnp.concatenate([low, block, high], axis=dim)
    return block


def masked_kernel(raw, sigma):
    offsets = jnp.arange(raw.shape[0]).astype(jnp.float32) - 7.0
    dist = offsets[:, None] ** 2 + offsets[None, :] ** 2
    mask = jnp.exp(-dist[:, :, None] / (2.0 * sigma[None, None, :] ** 2))
    return (raw * mask).astype(jnp.bfloat16)


def _dw_body(*refs, parts, taps, cbase, rows, cols, chans, rb):
    x_parts = refs[:parts]
    k_ref, o_all, xf_ref, xs_ref = refs[parts:]
    nlb = chans // 128
    njb = cols // 8
    nrb = rows // rb
    spread = max(1, min(8, 64 // (njb * nlb)))

    def one_strip(n, carry):
        o_ref = o_all.at[n]
        start = 0
        for x_all in x_parts:

            def widen_row(r, c, x_ref=x_all.at[n], start=start):
                xf_ref[start + r] = x_ref[r].astype(jnp.float32)
                return c

            lax.fori_loop(0, x_all.shape[1], widen_row, 0, unroll=spread)
            start += x_all.shape[1]
        first = True
        for s in range(8):
            if (cbase + s) % 8 == 0:
                src, off = xf_ref, cbase + s
            else:
                off = 0
                width = cols + 8 if s + 8 < taps else cols

                def shift(r, c, s=s, width=width):
                    xs_ref[r, pl.ds(0, width), :] = xf_ref[r, pl.ds(cbase + s, width), :]
                    return c

                lax.fori_loop(0, rows + taps - 1, shift, 0, unroll=spread)
                src = xs_ref
            for q in range(2):
                b = 8 * q + s
                if b >= taps:
                    continue
                for lb in range(nlb):
                    lanes = pl.ds(lb * 128, 128)
                    ks = [
                        jnp.broadcast_to(k_ref[a, pl.ds(b, 1), lanes], (8, 128))
                        for a in range(taps)
                    ]

                    def body(i, c, src=src, off=off, q=q, ks=ks, lanes=lanes, first=first):
                        r0 = pl.multiple_of((i // njb) * rb, rb)
                        j0 = pl.multiple_of((i % njb) * 8, 8)
                        xs = src[pl.ds(r0, rb + taps - 1), pl.ds(j0 + off + 8 * q, 8), lanes]
                        if first:
                            acc = jnp.zeros((rb, 8, 128), jnp.float32)
                        else:
                            acc = o_ref[pl.ds(r0, rb), pl.ds(j0, 8), lanes]
                        terms = [xs[a : a + rb] * ks[a][None] for a in range(taps)]
                        for g in range(0, taps, 5):
                            group = terms[g : g + 5]
                            while len(group) > 1:
                                group = [
                                    group[i] + group[i + 1] if i + 1 < len(group) else group[i]
                                    for i in range(0, len(group), 2)
                                ]
                            acc = acc + group[0]
                        o_ref[pl.ds(r0, rb), pl.ds(j0, 8), lanes] = acc
                        return c

                    lax.fori_loop(0, nrb * njb, body, 0, unroll=2)
                first = False
        return carry

    lax.fori_loop(0, x_parts[0].shape[0], one_strip, 0)


def depthwise(parts, kernel, cbase, cols):
    taps = kernel.shape[0]
    count = parts[0].shape[0]
    in_rows = sum(p.shape[1] for p in parts)
    rows = in_rows - taps + 1
    chans = parts[0].shape[3]
    body = functools.partial(
        _dw_body,
        parts=len(parts),
        taps=taps,
        cbase=cbase,
        rows=rows,
        cols=cols,
        chans=chans,
        rb=8,
    )
    vmem = pl.BlockSpec(memory_space=pltpu.VMEM)
    return pl.pallas_call(
        body,
        out_shape=jax.ShapeDtypeStruct((count, rows, cols, chans), jnp.float32),
        in_specs=[vmem] * (len(parts) + 1),
        out_specs=vmem,
        scratch_shapes=[
            pltpu.VMEM((in_rows,) + parts[0].shape[2:], jnp.float32),
            pltpu.VMEM((in_rows, cols + 8, chans), jnp.float32),
        ],
        cost_estimate=pl.CostEstimate(
            flops=2 * count * rows * cols * chans * taps * taps,
            transcendentals=0,
            bytes_accessed=sum(p.size for p in parts) * 2 + count * rows * cols * chans * 4,
        ),
    )(*parts, kernel.astype(jnp.float32))


def halos(block, axis, dim, width):
    count = lax.axis_size(axis)
    forward = [(i, i + 1) for i in range(count - 1)]
    backward = [(target, source) for source, target in forward]
    low = lax.ppermute(
        lax.slice_in_dim(block, block.shape[dim] - width, None, axis=dim), axis, forward
    )
    high = lax.ppermute(lax.slice_in_dim(block, 0, width, axis=dim), axis, backward)
    return low, high


def section_conv(block, kernel):
    reach = (kernel.shape[0] - 1) // 2
    cols = block.shape[1]
    band = 8
    up, down = halos(block, "row", 0, reach)
    pieces = [up, block, down]
    middle = depthwise([p[None] for p in pieces], kernel, band - reach, cols - 2 * band)

    def tall_cols(start, stop):
        return jnp.concatenate([p[:, start:stop] for p in pieces], axis=0)

    count = lax.axis_size("col")
    forward = [(i, i + 1) for i in range(count - 1)]
    backward = [(target, source) for source, target in forward]
    left = lax.ppermute(tall_cols(cols - reach, cols), "col", forward)
    right = lax.ppermute(tall_cols(0, reach), "col", backward)
    ends = jnp.stack(
        [
            jnp.concatenate([left, tall_cols(0, band + reach)], axis=1),
            jnp.concatenate([tall_cols(cols - band - reach, cols), right], axis=1),
        ],
        axis=0,
    )
    edge = depthwise([ends], kernel, 0, band)
    return jnp.concatenate([edge[0], middle[0], edge[1]], axis=1)


def local_section(field, raw, sigma, w_in, w_out):
    kernel = masked_kernel(raw, sigma)
    conv_out = section_conv(field, kernel)
    mean = jnp.mean(conv_out, axis=-1, keepdims=True)
    var = jnp.mean((conv_out - mean) ** 2, axis=-1, keepdims=True)
    normed = ((conv_out - mean) * lax.rsqrt(var + 1e-06)).astype(jnp.bfloat16)
    hidden = jax.nn.gelu(jnp.dot(normed, w_in, preferred_element_type=jnp.float32)).astype(
        jnp.bfloat16
    )
    mixed = jnp.dot(hidden, w_out, preferred_element_type=jnp.float32)
    return (field.astype(jnp.float32) + mixed).astype(jnp.bfloat16)


def blur_down(padded):
    rows = padded.shape[0] - 2
    cols = padded.shape[1] - 2
    padded = padded.astype(jnp.float32)
    upper = padded[0:rows].reshape(rows // 2, 2, cols + 2, -1)
    lower = padded[2 : rows + 2].reshape(rows // 2, 2, cols + 2, -1)
    vert = (upper[:, 0] + 3.0 * upper[:, 1] + 3.0 * lower[:, 0] + lower[:, 1]) / 8.0
    left = vert[:, 0:cols].reshape(rows // 2, cols // 2, 2, -1)
    right = vert[:, 2 : cols + 2].reshape(rows // 2, cols // 2, 2, -1)
    return (
        (left[:, :, 0] + 3.0 * left[:, :, 1] + 3.0 * right[:, :, 0] + right[:, :, 1]) / 8.0
    ).astype(jnp.bfloat16)


def on_device(
    image,
    raw_first,
    sigma_first,
    in_first,
    out_first,
    widen,
    raw_second,
    sigma_second,
    in_second,
    out_second,
):
    first = local_section(image, raw_first, sigma_first, in_first, out_first)
    first_cycle = padded_2(first, (("row", 0), ("col", 1)), 1)
    first_pooled = blur_down(first_cycle)
    widened = jnp.dot(first_pooled, widen, preferred_element_type=jnp.float32).astype(jnp.bfloat16)
    second = local_section(widened, raw_second, sigma_second, in_second, out_second)
    second_cycle = padded_2(second, (("row", 0), ("col", 1)), 1)
    return blur_down(second_cycle)


def solution(mesh):
    placed = (P("row", "col", None), P(), P(), P(), P(), P(), P(), P(), P(), P())
    return jax.shard_map(
        on_device, mesh=mesh, in_specs=placed, out_specs=P("row", "col", None), check_vma=False
    )
```

```python
import functools

import jax
import jax.numpy as jnp
from jax import lax
from jax.experimental import pallas as pl
from jax.experimental.pallas import tpu as pltpu
from jax.sharding import PartitionSpec as P


def padded_2(block, sides, width):
    for axis, dim in sides:
        count = lax.axis_size(axis)
        forward = [(i, i + 1) for i in range(count - 1)]
        backward = [(target, source) for source, target in forward]
        low = lax.ppermute(
            lax.slice_in_dim(block, block.shape[dim] - width, None, axis=dim), axis, forward
        )
        high = lax.ppermute(lax.slice_in_dim(block, 0, width, axis=dim), axis, backward)
        block = jnp.concatenate([low, block, high], axis=dim)
    return block


def masked_kernel(raw, sigma):
    offsets = jnp.arange(raw.shape[0]).astype(jnp.float32) - 7.0
    dist = offsets[:, None] ** 2 + offsets[None, :] ** 2
    mask = jnp.exp(-dist[:, :, None] / (2.0 * sigma[None, None, :] ** 2))
    return (raw * mask).astype(jnp.bfloat16)


def _dw_body(*refs, parts, taps, cbase, rows, cols, chans, rb):
    x_parts = refs[:parts]
    k_ref, o_all, xf_ref, xs_ref = refs[parts:]
    nlb = chans // 128
    njb = cols // 8
    nrb = rows // rb
    spread = max(1, min(16, 64 // (njb * nlb)))
    deep = 2

    def one_strip(n, carry):
        o_ref = o_all.at[n]
        start = 0
        for x_all in x_parts:

            def widen_row(r, c, x_ref=x_all.at[n], start=start):
                xf_ref[start + r] = x_ref[r].astype(jnp.float32)
                return c

            lax.fori_loop(0, x_all.shape[1], widen_row, 0, unroll=spread)
            start += x_all.shape[1]
        first = True
        for s in range(8):
            if (cbase + s) % 8 == 0:
                src, off = xf_ref, cbase + s
            else:
                off = 0
                width = cols + 8 if s + 8 < taps else cols

                def shift(r, c, s=s, width=width):
                    xs_ref[r, pl.ds(0, width), :] = xf_ref[r, pl.ds(cbase + s, width), :]
                    return c

                lax.fori_loop(0, rows + taps - 1, shift, 0, unroll=spread)
                src = xs_ref
            for q in range(2):
                b = 8 * q + s
                if b >= taps:
                    continue
                for lb in range(nlb):
                    lanes = pl.ds(lb * 128, 128)
                    ks = [
                        jnp.broadcast_to(k_ref[a, pl.ds(b, 1), lanes], (8, 128))
                        for a in range(taps)
                    ]

                    def body(i, c, src=src, off=off, q=q, ks=ks, lanes=lanes, first=first):
                        r0 = pl.multiple_of((i // njb) * rb, rb)
                        j0 = pl.multiple_of((i % njb) * 8, 8)
                        xs = src[pl.ds(r0, rb + taps - 1), pl.ds(j0 + off + 8 * q, 8), lanes]
                        if first:
                            acc = jnp.zeros((rb, 8, 128), jnp.float32)
                        else:
                            acc = o_ref[pl.ds(r0, rb), pl.ds(j0, 8), lanes]
                        terms = [xs[a : a + rb] * ks[a][None] for a in range(taps)]
                        for g in range(0, taps, 5):
                            group = terms[g : g + 5]
                            while len(group) > 1:
                                group = [
                                    group[i] + group[i + 1] if i + 1 < len(group) else group[i]
                                    for i in range(0, len(group), 2)
                                ]
                            acc = acc + group[0]
                        o_ref[pl.ds(r0, rb), pl.ds(j0, 8), lanes] = acc
                        return c

                    lax.fori_loop(0, nrb * njb, body, 0, unroll=deep)
                first = False
        return carry

    lax.fori_loop(0, x_parts[0].shape[0], one_strip, 0)


def depthwise(parts, kernel, cbase, cols):
    taps = kernel.shape[0]
    count = parts[0].shape[0]
    in_rows = sum(p.shape[1] for p in parts)
    rows = in_rows - taps + 1
    chans = parts[0].shape[3]
    body = functools.partial(
        _dw_body,
        parts=len(parts),
        taps=taps,
        cbase=cbase,
        rows=rows,
        cols=cols,
        chans=chans,
        rb=8,
    )
    vmem = pl.BlockSpec(memory_space=pltpu.VMEM)
    return pl.pallas_call(
        body,
        out_shape=jax.ShapeDtypeStruct((count, rows, cols, chans), jnp.float32),
        in_specs=[vmem] * (len(parts) + 1),
        out_specs=vmem,
        scratch_shapes=[
            pltpu.VMEM((in_rows,) + parts[0].shape[2:], jnp.float32),
            pltpu.VMEM((in_rows, cols + 8, chans), jnp.float32),
        ],
        cost_estimate=pl.CostEstimate(
            flops=2 * count * rows * cols * chans * taps * taps,
            transcendentals=0,
            bytes_accessed=sum(p.size for p in parts) * 2 + count * rows * cols * chans * 4,
        ),
    )(*parts, kernel.astype(jnp.float32))


def halos(block, axis, dim, width):
    count = lax.axis_size(axis)
    forward = [(i, i + 1) for i in range(count - 1)]
    backward = [(target, source) for source, target in forward]
    low = lax.ppermute(
        lax.slice_in_dim(block, block.shape[dim] - width, None, axis=dim), axis, forward
    )
    high = lax.ppermute(lax.slice_in_dim(block, 0, width, axis=dim), axis, backward)
    return low, high


def section_conv(block, kernel):
    reach = (kernel.shape[0] - 1) // 2
    cols = block.shape[1]
    band = 8
    up, down = halos(block, "row", 0, reach)
    pieces = [up, block, down]
    middle = depthwise([p[None] for p in pieces], kernel, band - reach, cols - 2 * band)

    def tall_cols(start, stop):
        return jnp.concatenate([p[:, start:stop] for p in pieces], axis=0)

    count = lax.axis_size("col")
    forward = [(i, i + 1) for i in range(count - 1)]
    backward = [(target, source) for source, target in forward]
    left = lax.ppermute(tall_cols(cols - reach, cols), "col", forward)
    right = lax.ppermute(tall_cols(0, reach), "col", backward)
    ends = jnp.stack(
        [
            jnp.concatenate([left, tall_cols(0, band + reach)], axis=1),
            jnp.concatenate([tall_cols(cols - band - reach, cols), right], axis=1),
        ],
        axis=0,
    )
    edge = depthwise([ends], kernel, 0, band)
    return jnp.concatenate([edge[0], middle[0], edge[1]], axis=1)


def local_section(field, raw, sigma, w_in, w_out):
    kernel = masked_kernel(raw, sigma)
    conv_out = section_conv(field, kernel)
    mean = jnp.mean(conv_out, axis=-1, keepdims=True)
    var = jnp.mean((conv_out - mean) ** 2, axis=-1, keepdims=True)
    normed = ((conv_out - mean) * lax.rsqrt(var + 1e-06)).astype(jnp.bfloat16)
    hidden = jax.nn.gelu(jnp.dot(normed, w_in, preferred_element_type=jnp.float32)).astype(
        jnp.bfloat16
    )
    mixed = jnp.dot(hidden, w_out, preferred_element_type=jnp.float32)
    return (field.astype(jnp.float32) + mixed).astype(jnp.bfloat16)


def blur_down(padded):
    rows = padded.shape[0] - 2
    cols = padded.shape[1] - 2
    padded = padded.astype(jnp.float32)
    upper = padded[0:rows].reshape(rows // 2, 2, cols + 2, -1)
    lower = padded[2 : rows + 2].reshape(rows // 2, 2, cols + 2, -1)
    vert = (upper[:, 0] + 3.0 * upper[:, 1] + 3.0 * lower[:, 0] + lower[:, 1]) / 8.0
    left = vert[:, 0:cols].reshape(rows // 2, cols // 2, 2, -1)
    right = vert[:, 2 : cols + 2].reshape(rows // 2, cols // 2, 2, -1)
    return (
        (left[:, :, 0] + 3.0 * left[:, :, 1] + 3.0 * right[:, :, 0] + right[:, :, 1]) / 8.0
    ).astype(jnp.bfloat16)


def on_device(
    image,
    raw_first,
    sigma_first,
    in_first,
    out_first,
    widen,
    raw_second,
    sigma_second,
    in_second,
    out_second,
):
    first = local_section(image, raw_first, sigma_first, in_first, out_first)
    first_cycle = padded_2(first, (("row", 0), ("col", 1)), 1)
    first_pooled = blur_down(first_cycle)
    widened = jnp.dot(first_pooled, widen, preferred_element_type=jnp.float32).astype(jnp.bfloat16)
    second = local_section(widened, raw_second, sigma_second, in_second, out_second)
    second_cycle = padded_2(second, (("row", 0), ("col", 1)), 1)
    return blur_down(second_cycle)


def solution(mesh):
    placed = (P("row", "col", None), P(), P(), P(), P(), P(), P(), P(), P(), P())
    return jax.shard_map(
        on_device, mesh=mesh, in_specs=placed, out_specs=P("row", "col", None), check_vma=False
    )
```

```python
import functools

import jax
import jax.numpy as jnp
from jax import lax
from jax.experimental import pallas as pl
from jax.experimental.pallas import tpu as pltpu
from jax.sharding import PartitionSpec as P


def padded_2(block, sides, width):
    for axis, dim in sides:
        count = lax.axis_size(axis)
        forward = [(i, i + 1) for i in range(count - 1)]
        backward = [(target, source) for source, target in forward]
        low = lax.ppermute(
            lax.slice_in_dim(block, block.shape[dim] - width, None, axis=dim), axis, forward
        )
        high = lax.ppermute(lax.slice_in_dim(block, 0, width, axis=dim), axis, backward)
        block = jnp.concatenate([low, block, high], axis=dim)
    return block


def masked_kernel(raw, sigma):
    offsets = jnp.arange(raw.shape[0]).astype(jnp.float32) - 7.0
    dist = offsets[:, None] ** 2 + offsets[None, :] ** 2
    mask = jnp.exp(-dist[:, :, None] / (2.0 * sigma[None, None, :] ** 2))
    return (raw * mask).astype(jnp.bfloat16)


def _dw_body(*refs, parts, taps, cbase, rows, cols, chans, rb):
    x_parts = refs[:parts]
    k_ref, o_all, xf_ref, xs_ref = refs[parts:]
    nlb = chans // 128
    njb = cols // 8
    nrb = rows // rb
    spread = max(1, min(8, 128 // (njb * nlb)))

    def one_strip(n, carry):
        o_ref = o_all.at[n]
        start = 0
        for x_all in x_parts:

            def widen_row(r, c, x_ref=x_all.at[n], start=start):
                xf_ref[start + r] = x_ref[r].astype(jnp.float32)
                return c

            lax.fori_loop(0, x_all.shape[1], widen_row, 0, unroll=spread)
            start += x_all.shape[1]
        first = True
        for s in range(8):
            if (cbase + s) % 8 == 0:
                src, off = xf_ref, cbase + s
            else:
                off = 0
                width = cols + 8 if s + 8 < taps else cols

                def shift(r, c, s=s, width=width):
                    xs_ref[r, pl.ds(0, width), :] = xf_ref[r, pl.ds(cbase + s, width), :]
                    return c

                lax.fori_loop(0, rows + taps - 1, shift, 0, unroll=spread)
                src = xs_ref
            for q in range(2):
                b = 8 * q + s
                if b >= taps:
                    continue
                for lb in range(nlb):
                    lanes = pl.ds(lb * 128, 128)
                    ks = [
                        jnp.broadcast_to(k_ref[a, pl.ds(b, 1), lanes], (8, 128))
                        for a in range(taps)
                    ]

                    def body(i, c, src=src, off=off, q=q, ks=ks, lanes=lanes, first=first):
                        r0 = pl.multiple_of((i // njb) * rb, rb)
                        j0 = pl.multiple_of((i % njb) * 8, 8)
                        xs = src[pl.ds(r0, rb + taps - 1), pl.ds(j0 + off + 8 * q, 8), lanes]
                        if first:
                            acc = jnp.zeros((rb, 8, 128), jnp.float32)
                        else:
                            acc = o_ref[pl.ds(r0, rb), pl.ds(j0, 8), lanes]
                        terms = [xs[a : a + rb] * ks[a][None] for a in range(taps)]
                        for g in range(0, taps, 5):
                            group = terms[g : g + 5]
                            while len(group) > 1:
                                group = [
                                    group[i] + group[i + 1] if i + 1 < len(group) else group[i]
                                    for i in range(0, len(group), 2)
                                ]
                            acc = acc + group[0]
                        o_ref[pl.ds(r0, rb), pl.ds(j0, 8), lanes] = acc
                        return c

                    lax.fori_loop(0, nrb * njb, body, 0, unroll=2)
                first = False
        return carry

    lax.fori_loop(0, x_parts[0].shape[0], one_strip, 0)


def depthwise(parts, kernel, cbase, cols):
    taps = kernel.shape[0]
    count = parts[0].shape[0]
    in_rows = sum(p.shape[1] for p in parts)
    rows = in_rows - taps + 1
    chans = parts[0].shape[3]
    body = functools.partial(
        _dw_body,
        parts=len(parts),
        taps=taps,
        cbase=cbase,
        rows=rows,
        cols=cols,
        chans=chans,
        rb=8,
    )
    vmem = pl.BlockSpec(memory_space=pltpu.VMEM)
    return pl.pallas_call(
        body,
        out_shape=jax.ShapeDtypeStruct((count, rows, cols, chans), jnp.float32),
        in_specs=[vmem] * (len(parts) + 1),
        out_specs=vmem,
        scratch_shapes=[
            pltpu.VMEM((in_rows,) + parts[0].shape[2:], jnp.float32),
            pltpu.VMEM((in_rows, cols + 8, chans), jnp.float32),
        ],
        cost_estimate=pl.CostEstimate(
            flops=2 * count * rows * cols * chans * taps * taps,
            transcendentals=0,
            bytes_accessed=sum(p.size for p in parts) * 2 + count * rows * cols * chans * 4,
        ),
    )(*parts, kernel.astype(jnp.float32))


def halos(block, axis, dim, width):
    count = lax.axis_size(axis)
    forward = [(i, i + 1) for i in range(count - 1)]
    backward = [(target, source) for source, target in forward]
    low = lax.ppermute(
        lax.slice_in_dim(block, block.shape[dim] - width, None, axis=dim), axis, forward
    )
    high = lax.ppermute(lax.slice_in_dim(block, 0, width, axis=dim), axis, backward)
    return low, high


def section_conv(block, kernel):
    reach = (kernel.shape[0] - 1) // 2
    cols = block.shape[1]
    band = 8
    up, down = halos(block, "row", 0, reach)
    pieces = [up, block, down]
    middle = depthwise([p[None] for p in pieces], kernel, band - reach, cols - 2 * band)

    def tall_cols(start, stop):
        return jnp.concatenate([p[:, start:stop] for p in pieces], axis=0)

    count = lax.axis_size("col")
    forward = [(i, i + 1) for i in range(count - 1)]
    backward = [(target, source) for source, target in forward]
    left = lax.ppermute(tall_cols(cols - reach, cols), "col", forward)
    right = lax.ppermute(tall_cols(0, reach), "col", backward)
    ends = jnp.stack(
        [
            jnp.concatenate([left, tall_cols(0, band + reach)], axis=1),
            jnp.concatenate([tall_cols(cols - band - reach, cols), right], axis=1),
        ],
        axis=0,
    )
    edge = depthwise([ends], kernel, 0, band)
    return jnp.concatenate([edge[0], middle[0], edge[1]], axis=1)


def local_section(field, raw, sigma, w_in, w_out):
    kernel = masked_kernel(raw, sigma)
    conv_out = section_conv(field, kernel)
    mean = jnp.mean(conv_out, axis=-1, keepdims=True)
    var = jnp.mean((conv_out - mean) ** 2, axis=-1, keepdims=True)
    normed = ((conv_out - mean) * lax.rsqrt(var + 1e-06)).astype(jnp.bfloat16)
    hidden = jax.nn.gelu(jnp.dot(normed, w_in, preferred_element_type=jnp.float32)).astype(
        jnp.bfloat16
    )
    mixed = jnp.dot(hidden, w_out, preferred_element_type=jnp.float32)
    return (field.astype(jnp.float32) + mixed).astype(jnp.bfloat16)


def blur_down(padded):
    rows = padded.shape[0] - 2
    cols = padded.shape[1] - 2
    padded = padded.astype(jnp.float32)
    upper = padded[0:rows].reshape(rows // 2, 2, cols + 2, -1)
    lower = padded[2 : rows + 2].reshape(rows // 2, 2, cols + 2, -1)
    vert = (upper[:, 0] + 3.0 * upper[:, 1] + 3.0 * lower[:, 0] + lower[:, 1]) / 8.0
    left = vert[:, 0:cols].reshape(rows // 2, cols // 2, 2, -1)
    right = vert[:, 2 : cols + 2].reshape(rows // 2, cols // 2, 2, -1)
    return (
        (left[:, :, 0] + 3.0 * left[:, :, 1] + 3.0 * right[:, :, 0] + right[:, :, 1]) / 8.0
    ).astype(jnp.bfloat16)


def on_device(
    image,
    raw_first,
    sigma_first,
    in_first,
    out_first,
    widen,
    raw_second,
    sigma_second,
    in_second,
    out_second,
):
    first = local_section(image, raw_first, sigma_first, in_first, out_first)
    first_cycle = padded_2(first, (("row", 0), ("col", 1)), 1)
    first_pooled = blur_down(first_cycle)
    widened = jnp.dot(first_pooled, widen, preferred_element_type=jnp.float32).astype(jnp.bfloat16)
    second = local_section(widened, raw_second, sigma_second, in_second, out_second)
    second_cycle = padded_2(second, (("row", 0), ("col", 1)), 1)
    return blur_down(second_cycle)


def solution(mesh):
    placed = (P("row", "col", None), P(), P(), P(), P(), P(), P(), P(), P(), P())
    return jax.shard_map(
        on_device, mesh=mesh, in_specs=placed, out_specs=P("row", "col", None), check_vma=False
    )
```
